128 devices in a mesh: expert: 16 (over y, x), etp: 8 (over z, core).
Axes of the slice: x: 4, y: 4, z: 4, core: 2. Of those that a mesh axis runs over, the one named last changes fastest.
Arguments:
- tokens: bfloat16 [2048, 2048], P('expert'), may hold values from -6 to 6
- out_grad: bfloat16 [2048, 2048], P('expert'), may hold values from -6 to 6
- routes: int32 [2048, 2], P('expert'), may hold values from 0 to 15, as said below
- combine_weights: float32 [2048, 2], P('expert'), may hold values from 0.2 to 1
- w_gate: bfloat16 [16, 2048, 7168], P('expert', None, 'etp'), may hold values from -0.125 to 0.125
- w_up: bfloat16 [16, 2048, 7168], P('expert', None, 'etp'), may hold values from -0.125 to 0.125
- w_down: bfloat16 [16, 7168, 2048], P('expert', 'etp'), may hold values from -0.0625 to 0.0625
Outputs:
- mixed: bfloat16 [2048, 2048], P('expert')
- tokens_grad: bfloat16 [2048, 2048], P('expert')
- combine_grad: float32 [2048, 2], P('expert')
- gate_weight_grad: bfloat16 [16, 2048, 7168], P('expert', None, 'etp')
- up_weight_grad: bfloat16 [16, 2048, 7168], P('expert', None, 'etp')
- down_weight_grad: bfloat16 [16, 7168, 2048], P('expert', 'etp')
The draws below stay inside these ranges and needn't reach their ends.
Inputs may be any that keep to these rules, and one draw needn't show every extreme that they name: `routes`: each token names two different experts. No expert is named by more than 32 tokens of one group of 128 consecutive tokens, and one expert, the same in every group, is named by exactly 32 tokens of each group.
All inputs are finite; a program needn't handle non-finite values.
Results may differ from the reference program's by a relative error of at most 0.02.
Values may be sent and summed in bfloat16 or wider, within the bound.
No kernel may reach another device: no remote copies, remote signals or barrier semaphores. Data moves between devices by JAX's collectives and lax.ppermute only.
A program may use at most 128 MiB of HBM per device.

```python
import jax
import jax.numpy as jnp
from jax import lax

D = 2048
FF_DEV = 896
TOP = 2
TOK_GRP = 128
EXPERTS = 16
BLOCKS = 8
FF = 7168
CAP = 32
TOKENS = 2048


def route_block(block_key, hot_expert):
    count_key, order_key, swap_key, token_key = jax.random.split(block_key, 4)
    weights = jax.random.randint(count_key, (EXPERTS - 1,), 2, 5)
    remaining = 2 * TOK_GRP - CAP
    base = jnp.minimum(remaining * weights // jnp.sum(weights), CAP)
    leftover = remaining - jnp.sum(base)
    room = CAP - base
    before = jnp.cumsum(room) - room
    extra = jnp.clip(leftover - before, 0, room)
    other_counts = base + extra
    order = jax.random.permutation(order_key, EXPERTS - 1)
    other_ids = (hot_expert + 1 + order) % EXPERTS
    run_ids = jnp.concatenate([jnp.reshape(hot_expert, (1,)), other_ids]).astype(jnp.int32)
    run_counts = jnp.concatenate([jnp.full((1,), CAP, jnp.int32), other_counts.astype(jnp.int32)])
    run_ends = jnp.cumsum(run_counts)
    positions = jnp.arange(2 * TOK_GRP, dtype=jnp.int32)
    run_index = jnp.sum((positions[:, None] >= run_ends[None, :]).astype(jnp.int32), axis=1)
    slot_ids = run_ids[run_index]
    paired = jnp.stack([slot_ids[:TOK_GRP], slot_ids[TOK_GRP:]], axis=1)
    swapped = jax.random.randint(swap_key, (TOK_GRP,), 0, 2)
    paired = jnp.where(swapped[:, None] == 1, paired[:, ::-1], paired)
    shuffle = jax.random.permutation(token_key, TOK_GRP)
    return paired[shuffle]


def draw_routes(key, part):
    group_count = TOKENS // TOK_GRP
    hot_key, rest_key = jax.random.split(jax.random.fold_in(key, 11))
    hot_expert = jax.random.randint(hot_key, (), 0, EXPERTS)
    block_keys = jax.random.split(rest_key, group_count)
    blocks = jax.vmap(lambda block_key: route_block(block_key, hot_expert))(block_keys)
    return blocks.reshape(TOKENS, TOP).astype(jnp.int32)


def block_scale(stream_key, dims, cuts, least, high):
    def one(dim, parts):
        heights = jax.random.uniform(jax.random.fold_in(jax.random.fold_in(stream_key, 6), dim), (parts,), jnp.float32, least / len(cuts), high / len(cuts))
        return jnp.repeat(jnp.exp(heights), dims[dim] // parts).reshape((-1,) + (1,) * (len(dims) - dim - 1))

    level = one(*cuts[0])
    for cut in cuts[1:]:
        level = level * one(*cut)
    return level


def noise(own_key, shape, width, bound, shards=(), held_as=jnp.bfloat16):
    loudness = block_scale(own_key, shape, shards, -0.22, 0.18) if shards else 1.0
    entries = jax.random.normal(own_key, shape, jnp.float32) * width * loudness
    return jnp.minimum(jnp.maximum(entries, -bound), bound).astype(held_as)


def setup_inputs(seed: int = 0) -> dict:
    keys = jax.random.split(jax.random.key(seed), 8)
    tokens = noise(keys[0], (TOKENS, D), 1.0, 6.0, ((0, 16),))
    out_grad = noise(keys[1], (TOKENS, D), 1.0, 6.0, ((0, 16),))
    routes = draw_routes(jax.random.fold_in(keys[7], 71), 0)
    combine_weights = jnp.clip(0.2 + 0.8 * jax.random.uniform(keys[3], (TOKENS, TOP), jnp.float32) ** block_scale(keys[3], (TOKENS, TOP), ((0, 16),), -0.2, 0.2), 0.2, 1.0)
    w_gate = noise(keys[4], (EXPERTS, D, FF), D ** -0.5, 0.125, ((0, 16), (2, 8)))
    w_up = noise(keys[5], (EXPERTS, D, FF), D ** -0.5, 0.125, ((0, 16), (2, 8)))
    w_down = noise(keys[6], (EXPERTS, FF, D), FF ** -0.5, 0.0625, ((0, 16), (1, 8)))
    return {"tokens": tokens, "out_grad": out_grad, "routes": routes, "combine_weights": combine_weights, "w_gate": w_gate, "w_up": w_up, "w_down": w_down}


def slot_numbers(routes):
    grouped = routes.reshape(TOKENS // TOK_GRP, TOK_GRP * TOP)
    one_hot = (grouped[:, :, None] == jnp.arange(EXPERTS, dtype=jnp.int32)[None, None, :]).astype(jnp.int32)
    before = jnp.cumsum(one_hot, axis=1) - one_hot
    return jnp.sum(before * one_hot, axis=2).reshape(TOKENS, TOP)


def expert_pass(operands):
    rows_in, rows_grad, gate_w, up_w, down_w = operands
    row_count = rows_in.shape[0]
    gate_pre = jnp.dot(rows_in, gate_w, preferred_element_type=jnp.float32)
    up_pre = jnp.dot(rows_in, up_w, preferred_element_type=jnp.float32)
    gate_sig = jax.nn.sigmoid(gate_pre)
    swish = gate_pre * gate_sig
    hidden = (swish * up_pre).astype(jnp.bfloat16)

    def add_out(block, total):
        start = block * FF_DEV
        hidden_block = lax.dynamic_slice_in_dim(hidden, start, FF_DEV, 1)
        down_block = lax.dynamic_slice_in_dim(down_w, start, FF_DEV, 0)
        term = jnp.dot(hidden_block, down_block, preferred_element_type=jnp.float32)
        return total + lax.optimization_barrier(term.astype(jnp.bfloat16)).astype(jnp.float32)

    out_total = lax.fori_loop(0, BLOCKS, add_out, jnp.zeros((row_count, D), jnp.float32))
    hidden_grad = jnp.dot(rows_grad, down_w.T, preferred_element_type=jnp.float32)
    down_grad = jnp.dot(hidden.T, rows_grad, preferred_element_type=jnp.float32).astype(jnp.bfloat16)
    gate_grad = (hidden_grad * up_pre * gate_sig * (1.0 + gate_pre * (1.0 - gate_sig))).astype(jnp.bfloat16)
    up_grad = (hidden_grad * swish).astype(jnp.bfloat16)
    gate_weight_grad = jnp.dot(rows_in.T, gate_grad, preferred_element_type=jnp.float32).astype(jnp.bfloat16)
    up_weight_grad = jnp.dot(rows_in.T, up_grad, preferred_element_type=jnp.float32).astype(jnp.bfloat16)

    def add_input(block, total):
        start = block * FF_DEV
        gate_block = lax.dynamic_slice_in_dim(gate_grad, start, FF_DEV, 1)
        up_block = lax.dynamic_slice_in_dim(up_grad, start, FF_DEV, 1)
        gate_cols = lax.dynamic_slice_in_dim(gate_w, start, FF_DEV, 1)
        up_cols = lax.dynamic_slice_in_dim(up_w, start, FF_DEV, 1)
        term = jnp.dot(gate_block, gate_cols.T, preferred_element_type=jnp.float32)
        term = term + jnp.dot(up_block, up_cols.T, preferred_element_type=jnp.float32)
        return total + lax.optimization_barrier(term.astype(jnp.bfloat16)).astype(jnp.float32)

    input_total = lax.fori_loop(0, BLOCKS, add_input, jnp.zeros((row_count, D), jnp.float32))
    return (out_total.astype(jnp.bfloat16), input_total.astype(jnp.bfloat16),
            gate_weight_grad, up_weight_grad, down_grad)


def reference(tokens, out_grad, routes, combine_weights, w_gate, w_up, w_down):
    slots = slot_numbers(routes)
    group_of = (jnp.arange(TOKENS, dtype=jnp.int32) // TOK_GRP)[:, None]
    expert_rows = EXPERTS * CAP
    position = (routes * expert_rows + group_of * CAP + slots).astype(jnp.int32)
    pair_count = TOKENS * TOP
    source_index = jnp.full((EXPERTS * expert_rows,), pair_count, jnp.int32)
    source_index = source_index.at[position.reshape(-1)].set(jnp.arange(pair_count, dtype=jnp.int32))
    zero_row = jnp.zeros((1, D), jnp.bfloat16)
    padded_tokens = jnp.concatenate([tokens, zero_row], axis=0)
    scaled_grad = (combine_weights[:, :, None] * out_grad.astype(jnp.float32)[:, None, :]).astype(jnp.bfloat16)
    padded_grad = jnp.concatenate([scaled_grad.reshape(pair_count, D), zero_row], axis=0)
    rows_in = padded_tokens[source_index // TOP].reshape(EXPERTS, expert_rows, D)
    rows_grad = padded_grad[source_index].reshape(EXPERTS, expert_rows, D)
    out_rows, input_rows, gate_weight_grad, up_weight_grad, down_weight_grad = lax.map(
        expert_pass, (rows_in, rows_grad, w_gate, w_up, w_down))
    out_pairs = out_rows.reshape(EXPERTS * expert_rows, D)[position].astype(jnp.float32)
    input_pairs = input_rows.reshape(EXPERTS * expert_rows, D)[position].astype(jnp.float32)
    mixed = jnp.sum(combine_weights[:, :, None] * out_pairs, axis=1).astype(jnp.bfloat16)
    combine_grad = jnp.sum(out_grad.astype(jnp.float32)[:, None, :] * out_pairs, axis=2)
    tokens_grad = jnp.sum(input_pairs, axis=1).astype(jnp.bfloat16)
    return (mixed, tokens_grad, combine_grad, gate_weight_grad, up_weight_grad, down_weight_grad)
```

```python
import jax
import jax.numpy as jnp
from jax import lax
from jax.sharding import PartitionSpec as P

TOP = 2


def contract_last(left, right):
    return lax.dot_general(
        left, right, (((1,), (1,)), ((), ())), preferred_element_type=jnp.float32
    )


def contract_first(left, right):
    return lax.dot_general(
        left, right, (((0,), (0,)), ((), ())), preferred_element_type=jnp.float32
    )


def select_rows(selector, table):
    return jnp.dot(selector.astype(table.dtype), table, preferred_element_type=jnp.float32)


def expert_pass(rows_in, rows_grad, gate_w, up_w, down_w):
    gate_pre = jnp.dot(rows_in, gate_w, preferred_element_type=jnp.float32)
    up_pre = jnp.dot(rows_in, up_w, preferred_element_type=jnp.float32)
    gate_sig = jax.nn.sigmoid(gate_pre)
    swish = gate_pre * gate_sig
    hidden = (swish * up_pre).astype(jnp.bfloat16)
    out_part = jnp.dot(hidden, down_w, preferred_element_type=jnp.float32)
    hidden_grad = contract_last(rows_grad, down_w)
    down_grad = contract_first(hidden, rows_grad).astype(jnp.bfloat16)
    gate_grad = (hidden_grad * up_pre * gate_sig * (1.0 + gate_pre * (1.0 - gate_sig))).astype(
        jnp.bfloat16
    )
    up_grad = (hidden_grad * swish).astype(jnp.bfloat16)
    gate_weight_grad = contract_first(rows_in, gate_grad).astype(jnp.bfloat16)
    up_weight_grad = contract_first(rows_in, up_grad).astype(jnp.bfloat16)
    input_part = contract_last(gate_grad, gate_w) + contract_last(up_grad, up_w)
    return (out_part, input_part, gate_weight_grad, up_weight_grad, down_grad)


def shards(tokens, out_grad, routes, combine_weights, w_gate, w_up, w_down):
    expert_count = lax.axis_size("expert")
    split_count = lax.axis_size("etp")
    me = lax.axis_index("etp")
    token_count, features = tokens.shape
    capacity = token_count // 4
    per_split = capacity // split_count
    pair_count = token_count * TOP

    flat_routes = routes.reshape(pair_count)
    expert_hot = (flat_routes[:, None] == jnp.arange(expert_count, dtype=jnp.int32)[None, :]).astype(
        jnp.int32
    )
    before = jnp.cumsum(expert_hot, axis=0) - expert_hot
    slots = jnp.sum(before * expert_hot, axis=1)

    mine = (slots // per_split) == me
    local_place = jnp.where(mine, flat_routes * per_split + slots % per_split, -1)
    place_count = expert_count * per_split
    pick = local_place[None, :] == jnp.arange(place_count, dtype=jnp.int32)[:, None]
    pick_tokens = jnp.any(pick.reshape(place_count, token_count, TOP), axis=2)

    scaled_grad = (combine_weights[:, :, None] * out_grad.astype(jnp.float32)[:, None, :]).astype(
        jnp.bfloat16
    )
    send_rows = select_rows(pick_tokens, tokens).astype(jnp.bfloat16)
    send_grad = select_rows(pick, scaled_grad.reshape(pair_count, features)).astype(jnp.bfloat16)
    send = jnp.concatenate(
        [
            send_rows.reshape(expert_count, per_split, features),
            send_grad.reshape(expert_count, per_split, features),
        ],
        axis=1,
    )
    recv = lax.all_to_all(send, "expert", split_axis=0, concat_axis=0, tiled=True)
    rows_in = lax.all_gather(recv[:, :per_split], "etp", axis=0, tiled=False).reshape(
        split_count * expert_count * per_split, features
    )
    rows_grad = lax.all_gather(recv[:, per_split:], "etp", axis=0, tiled=False).reshape(
        split_count * expert_count * per_split, features
    )

    out_part, input_part, gate_weight_grad, up_weight_grad, down_weight_grad = expert_pass(
        rows_in, rows_grad, w_gate[0], w_up[0], w_down[0]
    )
    out_sum = lax.psum_scatter(out_part.astype(jnp.bfloat16), "etp", scatter_dimension=0, tiled=True)
    input_sum = lax.psum_scatter(
        input_part.astype(jnp.bfloat16), "etp", scatter_dimension=0, tiled=True
    )
    back = jnp.concatenate(
        [
            out_sum.reshape(expert_count, per_split, features),
            input_sum.reshape(expert_count, per_split, features),
        ],
        axis=1,
    )
    back = lax.all_to_all(back, "expert", split_axis=0, concat_axis=0, tiled=True)
    out_table = back[:, :per_split].reshape(place_count, features)
    input_table = back[:, per_split:].reshape(place_count, features)

    gather = pick.T
    out_pairs = select_rows(gather, out_table).reshape(token_count, TOP, features)
    input_pairs = select_rows(gather, input_table).reshape(token_count, TOP, features)
    grad_values = out_grad.astype(jnp.float32)
    mixed_part = jnp.sum(combine_weights[:, :, None] * out_pairs, axis=1)
    tokens_part = jnp.sum(input_pairs, axis=1)
    combine_part = jnp.sum(grad_values[:, None, :] * out_pairs, axis=2)
    combine_high = combine_part.astype(jnp.bfloat16)
    combine_low = (combine_part - combine_high.astype(jnp.float32)).astype(jnp.bfloat16)
    pad = jnp.zeros((token_count, 128 - 2 * TOP), jnp.bfloat16)
    packed = jnp.concatenate(
        [
            mixed_part.astype(jnp.bfloat16),
            tokens_part.astype(jnp.bfloat16),
            combine_high,
            combine_low,
            pad,
        ],
        axis=1,
    )
    total = lax.psum(packed, "etp")
    mixed = total[:, :features]
    tokens_grad = total[:, features : 2 * features]
    combine_grad = total[:, 2 * features : 2 * features + TOP].astype(jnp.float32) + total[
        :, 2 * features + TOP : 2 * features + 2 * TOP
    ].astype(jnp.float32)
    return (
        mixed,
        tokens_grad,
        combine_grad,
        gate_weight_grad[None],
        up_weight_grad[None],
        down_weight_grad[None],
    )


def solution(mesh):
    return jax.shard_map(
        shards,
        mesh=mesh,
        in_specs=(
            P("expert", None),
            P("expert", None),
            P("expert", None),
            P("expert", None),
            P("expert", None, "etp"),
            P("expert", None, "etp"),
            P("expert", "etp", None),
        ),
        out_specs=(
            P("expert", None),
            P("expert", None),
            P("expert", None),
            P("expert", None, "etp"),
            P("expert", None, "etp"),
            P("expert", "etp", None),
        ),
        check_vma=False,
    )
```

```python
import jax
import jax.numpy as jnp
from jax import lax
from jax.sharding import PartitionSpec as P

TOP = 2


def contract_last(left, right):
    return lax.dot_general(
        left, right, (((1,), (1,)), ((), ())), preferred_element_type=jnp.float32
    )


def contract_first(left, right):
    return lax.dot_general(
        left, right, (((0,), (0,)), ((), ())), preferred_element_type=jnp.float32
    )


def select_rows(selector, table):
    return jnp.dot(selector.astype(table.dtype), table, preferred_element_type=jnp.float32)


def expert_pass(rows_in, rows_grad, gate_w, up_w, down_w):
    gate_pre = jnp.dot(rows_in, gate_w, preferred_element_type=jnp.float32)
    up_pre = jnp.dot(rows_in, up_w, preferred_element_type=jnp.float32)
    gate_sig = jax.nn.sigmoid(gate_pre)
    swish = gate_pre * gate_sig
    hidden = (swish * up_pre).astype(jnp.bfloat16)
    out_part = jnp.dot(hidden, down_w, preferred_element_type=jnp.float32)
    hidden_grad = contract_last(rows_grad, down_w)
    down_grad = contract_first(hidden, rows_grad).astype(jnp.bfloat16)
    gate_grad = (hidden_grad * up_pre * gate_sig * (1.0 + gate_pre * (1.0 - gate_sig))).astype(
        jnp.bfloat16
    )
    up_grad = (hidden_grad * swish).astype(jnp.bfloat16)
    gate_weight_grad = contract_first(rows_in, gate_grad).astype(jnp.bfloat16)
    up_weight_grad = contract_first(rows_in, up_grad).astype(jnp.bfloat16)
    input_part = contract_last(gate_grad, gate_w) + contract_last(up_grad, up_w)
    return (out_part, input_part, gate_weight_grad, up_weight_grad, down_grad)


def etp_perms(split_count):
    up = [(i, (i + 2) % split_count) for i in range(split_count)]
    down = [(i, (i - 2) % split_count) for i in range(split_count)]
    partner = [(i, i ^ 1) for i in range(split_count)]
    return up, down, partner


def etp_gather(lower, upper, split_count):
    up, down, partner = etp_perms(split_count)
    ring = split_count // 2
    lowers, uppers = [lower], [upper]
    for _ in range(ring - 1):
        lower = lax.ppermute(lower, "etp", up)
        upper = lax.ppermute(upper, "etp", down)
        lowers.append(lower)
        uppers.append(upper)
    chip = jnp.stack(lowers + uppers, axis=1)
    other = lax.ppermute(chip, "etp", partner)
    return jnp.stack([chip, other], axis=1)


def etp_reduce(part, split_count):
    up, down, partner = etp_perms(split_count)
    ring = split_count // 2
    part = part.astype(jnp.bfloat16)
    from_partner = lax.ppermute(part[1], "etp", partner)
    chip = part[0].astype(jnp.float32) + from_partner.astype(jnp.float32)
    lower = chip[1]
    upper = chip[ring + 1]
    for step in range(2, ring):
        lower = lax.ppermute(lower.astype(jnp.bfloat16), "etp", up).astype(jnp.float32) + chip[step]
        upper = (
            lax.ppermute(upper.astype(jnp.bfloat16), "etp", down).astype(jnp.float32)
            + chip[ring + step]
        )
    lower = lax.ppermute(lower.astype(jnp.bfloat16), "etp", up).astype(jnp.float32) + chip[0]
    upper = lax.ppermute(upper.astype(jnp.bfloat16), "etp", down).astype(jnp.float32) + chip[ring]
    return jnp.stack([lower, upper], axis=0)


def shards(tokens, out_grad, routes, combine_weights, w_gate, w_up, w_down):
    expert_count = lax.axis_size("expert")
    split_count = lax.axis_size("etp")
    ring = split_count // 2
    me = lax.axis_index("etp")
    my_z = me // 2
    my_core = me % 2
    token_count, features = tokens.shape
    capacity = token_count // 4
    per_split = capacity // split_count
    pair_count = token_count * TOP
    half = expert_count // 2

    flat_routes = routes.reshape(pair_count)
    expert_hot = (flat_routes[:, None] == jnp.arange(expert_count, dtype=jnp.int32)[None, :]).astype(
        jnp.int32
    )
    before = jnp.cumsum(expert_hot, axis=0) - expert_hot
    slots = jnp.sum(before * expert_hot, axis=1)

    mine = (slots // per_split) == me
    local_place = jnp.where(mine, flat_routes * per_split + slots % per_split, -1)
    place_count = expert_count * per_split
    pick = local_place[None, :] == jnp.arange(place_count, dtype=jnp.int32)[:, None]
    pick_tokens = jnp.any(pick.reshape(place_count, token_count, TOP), axis=2)

    scaled_grad = (combine_weights[:, :, None] * out_grad.astype(jnp.float32)[:, None, :]).astype(
        jnp.bfloat16
    )
    send_rows = select_rows(pick_tokens, tokens).astype(jnp.bfloat16)
    send_grad = select_rows(pick, scaled_grad.reshape(pair_count, features)).astype(jnp.bfloat16)
    send = jnp.concatenate(
        [
            send_rows.reshape(expert_count, per_split, features),
            send_grad.reshape(expert_count, per_split, features),
        ],
        axis=1,
    )
    recv = lax.all_to_all(send, "expert", split_axis=0, concat_axis=0, tiled=True)
    recv = recv.reshape(expert_count, 2, per_split, features).transpose(1, 0, 2, 3)
    gathered = etp_gather(recv[:, :half], recv[:, half:], split_count)
    row_total = split_count * expert_count * per_split
    rows_in = gathered[0].reshape(row_total, features)
    rows_grad = gathered[1].reshape(row_total, features)

    out_part, input_part, gate_weight_grad, up_weight_grad, down_weight_grad = expert_pass(
        rows_in, rows_grad, w_gate[0], w_up[0], w_down[0]
    )
    block = (2, 2 * ring, half * per_split, features)
    out_sum = etp_reduce(out_part.reshape(block), split_count)
    input_sum = etp_reduce(input_part.reshape(block), split_count)
    back = jnp.concatenate(
        [
            out_sum.astype(jnp.bfloat16).reshape(expert_count, per_split, features),
            input_sum.astype(jnp.bfloat16).reshape(expert_count, per_split, features),
        ],
        axis=1,
    )
    back = lax.all_to_all(back, "expert", split_axis=0, concat_axis=0, tiled=True)
    back = back.reshape(expert_count, 2, per_split, features).transpose(1, 0, 2, 3)
    tables = etp_gather(back[:, :half], back[:, half:], split_count)
    out_table = tables[0].reshape(row_total, features)
    input_table = tables[1].reshape(row_total, features)

    source = slots // per_split
    source_z = source // 2
    core_rel = (source % 2) ^ my_core
    is_upper = flat_routes // half
    offset = jnp.where(is_upper == 1, source_z - my_z, my_z - source_z) % ring
    table_row = (
        ((core_rel * 2 + is_upper) * ring + offset) * half + flat_routes % half
    ) * per_split + slots % per_split
    gather = table_row[:, None] == jnp.arange(row_total, dtype=jnp.int32)[None, :]
    out_pairs = select_rows(gather, out_table).reshape(token_count, TOP, features)
    input_pairs = select_rows(gather, input_table).reshape(token_count, TOP, features)
    grad_values = out_grad.astype(jnp.float32)
    mixed = jnp.sum(combine_weights[:, :, None] * out_pairs, axis=1).astype(jnp.bfloat16)
    combine_grad = jnp.sum(grad_values[:, None, :] * out_pairs, axis=2)
    tokens_grad = jnp.sum(input_pairs, axis=1).astype(jnp.bfloat16)
    return (
        mixed,
        tokens_grad,
        combine_grad,
        gate_weight_grad[None],
        up_weight_grad[None],
        down_weight_grad[None],
    )


def solution(mesh):
    return jax.shard_map(
        shards,
        mesh=mesh,
        in_specs=(
            P("expert", None),
            P("expert", None),
            P("expert", None),
            P("expert", None),
            P("expert", None, "etp"),
            P("expert", None, "etp"),
            P("expert", "etp", None),
        ),
        out_specs=(
            P("expert", None),
            P("expert", None),
            P("expert", None),
            P("expert", None, "etp"),
            P("expert", None, "etp"),
            P("expert", "etp", None),
        ),
        check_vma=False,
    )
```

```python
import jax
import jax.numpy as jnp
from jax import lax
from jax.sharding import PartitionSpec as P

TOP = 2


def contract_last(left, right):
    return lax.dot_general(
        left, right, (((1,), (1,)), ((), ())), preferred_element_type=jnp.float32
    )


def contract_first(left, right):
    return lax.dot_general(
        left, right, (((0,), (0,)), ((), ())), preferred_element_type=jnp.float32
    )


def select_rows(selector, table):
    return jnp.dot(selector.astype(table.dtype), table, preferred_element_type=jnp.float32)


def expert_pass(rows_in, rows_grad, gate_w, up_w, down_w):
    gate_pre = jnp.dot(rows_in, gate_w, preferred_element_type=jnp.float32)
    up_pre = jnp.dot(rows_in, up_w, preferred_element_type=jnp.float32)
    gate_sig = jax.nn.sigmoid(gate_pre)
    swish = gate_pre * gate_sig
    hidden = (swish * up_pre).astype(jnp.bfloat16)
    out_part = jnp.dot(hidden, down_w, preferred_element_type=jnp.float32)
    hidden_grad = contract_last(rows_grad, down_w)
    down_grad = contract_first(hidden, rows_grad).astype(jnp.bfloat16)
    gate_grad = (hidden_grad * up_pre * gate_sig * (1.0 + gate_pre * (1.0 - gate_sig))).astype(
        jnp.bfloat16
    )
    up_grad = (hidden_grad * swish).astype(jnp.bfloat16)
    gate_weight_grad = contract_first(rows_in, gate_grad).astype(jnp.bfloat16)
    up_weight_grad = contract_first(rows_in, up_grad).astype(jnp.bfloat16)
    input_part = contract_last(gate_grad, gate_w) + contract_last(up_grad, up_w)
    return (out_part, input_part, gate_weight_grad, up_weight_grad, down_grad)


def etp_perms(split_count):
    up = [(i, (i + 2) % split_count) for i in range(split_count)]
    down = [(i, (i - 2) % split_count) for i in range(split_count)]
    partner = [(i, i ^ 1) for i in range(split_count)]
    return up, down, partner


def etp_gather(lower, upper, split_count):
    up, down, partner = etp_perms(split_count)
    ring = split_count // 2
    lowers, uppers = [lower], [upper]
    for _ in range(ring - 1):
        lower = lax.ppermute(lower, "etp", up)
        upper = lax.ppermute(upper, "etp", down)
        lowers.append(lower)
        uppers.append(upper)
    chip = jnp.stack(lowers + uppers, axis=1)
    other = lax.ppermute(chip, "etp", partner)
    return jnp.stack([chip, other], axis=1)


def etp_reduce(part, split_count):
    up, down, partner = etp_perms(split_count)
    ring = split_count // 2
    part = part.astype(jnp.bfloat16)
    from_partner = lax.ppermute(part[1], "etp", partner)
    chip = part[0].astype(jnp.float32) + from_partner.astype(jnp.float32)
    lower = chip[1]
    upper = chip[ring + 1]
    for step in range(2, ring):
        lower = lax.ppermute(lower.astype(jnp.bfloat16), "etp", up).astype(jnp.float32) + chip[step]
        upper = (
            lax.ppermute(upper.astype(jnp.bfloat16), "etp", down).astype(jnp.float32)
            + chip[ring + step]
        )
    lower = lax.ppermute(lower.astype(jnp.bfloat16), "etp", up).astype(jnp.float32) + chip[0]
    upper = lax.ppermute(upper.astype(jnp.bfloat16), "etp", down).astype(jnp.float32) + chip[ring]
    return jnp.stack([lower, upper], axis=0)


def torus_shape(expert_count):
    across = int(round(expert_count**0.5))
    while expert_count % across:
        across -= 1
    return expert_count // across, across


def expert_exchange(chunks, expert_count, inverse):
    rows, cols = torus_shape(expert_count)
    arrived = [chunks[0]]
    for offset in range(1, expert_count):
        dy, dx = divmod(offset, cols)
        if inverse:
            dy, dx = -dy, -dx
        perm = [
            (e, ((e // cols + dy) % rows) * cols + (e % cols + dx) % cols)
            for e in range(expert_count)
        ]
        arrived.append(lax.ppermute(chunks[offset], "expert", perm))
    return jnp.stack(arrived, axis=0)


def shards(tokens, out_grad, routes, combine_weights, w_gate, w_up, w_down):
    expert_count = lax.axis_size("expert")
    split_count = lax.axis_size("etp")
    ring = split_count // 2
    me = lax.axis_index("etp")
    torus_rows, torus_cols = torus_shape(expert_count)
    my_expert = lax.axis_index("expert")
    my_z = me // 2
    my_core = me % 2
    token_count, features = tokens.shape
    capacity = token_count // 4
    per_split = capacity // split_count
    pair_count = token_count * TOP
    half = expert_count // 2

    flat_routes = routes.reshape(pair_count)
    expert_hot = (flat_routes[:, None] == jnp.arange(expert_count, dtype=jnp.int32)[None, :]).astype(
        jnp.int32
    )
    before = jnp.cumsum(expert_hot, axis=0) - expert_hot
    slots = jnp.sum(before * expert_hot, axis=1)

    route_offset = ((flat_routes // torus_cols - my_expert // torus_cols) % torus_rows) * torus_cols + (
        flat_routes % torus_cols - my_expert % torus_cols
    ) % torus_cols

    mine = (slots // per_split) == me
    local_place = jnp.where(mine, route_offset * per_split + slots % per_split, -1)
    place_count = expert_count * per_split
    pick = local_place[None, :] == jnp.arange(place_count, dtype=jnp.int32)[:, None]
    pick_tokens = jnp.any(pick.reshape(place_count, token_count, TOP), axis=2)

    scaled_grad = (combine_weights[:, :, None] * out_grad.astype(jnp.float32)[:, None, :]).astype(
        jnp.bfloat16
    )
    send_rows = select_rows(pick_tokens, tokens).astype(jnp.bfloat16)
    send_grad = select_rows(pick, scaled_grad.reshape(pair_count, features)).astype(jnp.bfloat16)
    send = jnp.concatenate(
        [
            send_rows.reshape(expert_count, per_split, features),
            send_grad.reshape(expert_count, per_split, features),
        ],
        axis=1,
    )
    recv = expert_exchange(send, expert_count, False)
    recv = recv.reshape(expert_count, 2, per_split, features).transpose(1, 0, 2, 3)
    recv = recv.reshape(2, expert_count * per_split, features)
    gathered = etp_gather(recv[:, : half * per_split], recv[:, half * per_split :], split_count)
    row_total = split_count * expert_count * per_split
    rows_in = gathered[0].reshape(row_total, features)
    rows_grad = gathered[1].reshape(row_total, features)

    out_part, input_part, gate_weight_grad, up_weight_grad, down_weight_grad = expert_pass(
        rows_in, rows_grad, w_gate[0], w_up[0], w_down[0]
    )
    block = (2, 2 * ring, half * per_split, features)
    out_sum = etp_reduce(out_part.reshape(block), split_count)
    input_sum = etp_reduce(input_part.reshape(block), split_count)
    back = jnp.concatenate(
        [
            out_sum.astype(jnp.bfloat16).reshape(expert_count, per_split, features),
            input_sum.astype(jnp.bfloat16).reshape(expert_count, per_split, features),
        ],
        axis=1,
    )
    back = expert_exchange(back, expert_count, True)
    back = back.reshape(expert_count, 2, per_split, features).transpose(1, 0, 2, 3)
    back = back.reshape(2, expert_count * per_split, features)
    tables = etp_gather(back[:, : half * per_split], back[:, half * per_split :], split_count)
    out_table = tables[0].reshape(row_total, features)
    input_table = tables[1].reshape(row_total, features)

    source = slots // per_split
    source_z = source // 2
    core_rel = (source % 2) ^ my_core
    is_upper = route_offset // half
    offset = jnp.where(is_upper == 1, source_z - my_z, my_z - source_z) % ring
    table_row = (
        ((core_rel * 2 + is_upper) * ring + offset) * half + route_offset % half
    ) * per_split + slots % per_split
    gather = table_row[:, None] == jnp.arange(row_total, dtype=jnp.int32)[None, :]
    out_pairs = select_rows(gather, out_table).reshape(token_count, TOP, features)
    input_pairs = select_rows(gather, input_table).reshape(token_count, TOP, features)
    grad_values = out_grad.astype(jnp.float32)
    mixed = jnp.sum(combine_weights[:, :, None] * out_pairs, axis=1).astype(jnp.bfloat16)
    combine_grad = jnp.sum(grad_values[:, None, :] * out_pairs, axis=2)
    tokens_grad = jnp.sum(input_pairs, axis=1).astype(jnp.bfloat16)
    return (
        mixed,
        tokens_grad,
        combine_grad,
        gate_weight_grad[None],
        up_weight_grad[None],
        down_weight_grad[None],
    )


def solution(mesh):
    return jax.shard_map(
        shards,
        mesh=mesh,
        in_specs=(
            P("expert", None),
            P("expert", None),
            P("expert", None),
            P("expert", None),
            P("expert", None, "etp"),
            P("expert", None, "etp"),
            P("expert", "etp", None),
        ),
        out_specs=(
            P("expert", None),
            P("expert", None),
            P("expert", None),
            P("expert", None, "etp"),
            P("expert", None, "etp"),
            P("expert", "etp", None),
        ),
        check_vma=False,
    )
```

```python
import jax
import jax.numpy as jnp
from jax import lax
from jax.sharding import PartitionSpec as P

TOP = 2


def contract_last(left, right):
    return lax.dot_general(
        left, right, (((1,), (1,)), ((), ())), preferred_element_type=jnp.float32
    )


def contract_first(left, right):
    return lax.dot_general(
        left, right, (((0,), (0,)), ((), ())), preferred_element_type=jnp.float32
    )


def select_rows(selector, table):
    return jnp.dot(selector.astype(table.dtype), table, preferred_element_type=jnp.float32)


def expert_pass(rows_in, rows_grad, gate_w, up_w, down_w):
    gate_pre = jnp.dot(rows_in, gate_w, preferred_element_type=jnp.float32)
    up_pre = jnp.dot(rows_in, up_w, preferred_element_type=jnp.float32)
    gate_sig = jax.nn.sigmoid(gate_pre)
    swish = gate_pre * gate_sig
    hidden = (swish * up_pre).astype(jnp.bfloat16)
    out_part = jnp.dot(hidden, down_w, preferred_element_type=jnp.float32)
    hidden_grad = contract_last(rows_grad, down_w)
    down_grad = contract_first(hidden, rows_grad).astype(jnp.bfloat16)
    gate_grad = (hidden_grad * up_pre * gate_sig * (1.0 + gate_pre * (1.0 - gate_sig))).astype(
        jnp.bfloat16
    )
    up_grad = (hidden_grad * swish).astype(jnp.bfloat16)
    gate_weight_grad = contract_first(rows_in, gate_grad).astype(jnp.bfloat16)
    up_weight_grad = contract_first(rows_in, up_grad).astype(jnp.bfloat16)
    input_part = contract_last(gate_grad, gate_w) + contract_last(up_grad, up_w)
    return (out_part, input_part, gate_weight_grad, up_weight_grad, down_grad)


SLOT_OF = ((0, 1), (2, 3), (4, 7), (6, 5))


def etp_perms(split_count):
    ring = split_count // 2
    swap = [(i, i ^ 1) for i in range(split_count)]
    onward = [(i, ((i // 2 + 1 - 2 * (i % 2)) % ring) * 2 + i % 2) for i in range(split_count)]
    backward = [(target, source) for source, target in onward]
    return swap, onward, backward


def etp_gather(unit, split_count):
    swap, onward, _ = etp_perms(split_count)
    chip = jnp.stack([unit, lax.ppermute(unit, "etp", swap)], axis=1)
    first = lax.ppermute(chip, "etp", onward)
    second = lax.ppermute(first[:, 0], "etp", onward)
    held = jnp.concatenate([first, second[:, None]], axis=1)
    other = lax.ppermute(held, "etp", swap)
    return jnp.concatenate([chip, held, other], axis=1)


def etp_reduce(part, split_count):
    swap, _, backward = etp_perms(split_count)

    def send(value, perm):
        return lax.ppermute(value.astype(jnp.bfloat16), "etp", perm).astype(jnp.float32)

    held = part[2:5] + send(part[5:8], swap)
    near = held[0] + send(held[2], backward)
    chip = part[0:2] + send(jnp.stack([near, held[1]], axis=0), backward)
    return chip[0] + send(chip[1], swap)


def shards(tokens, out_grad, routes, combine_weights, w_gate, w_up, w_down):
    expert_count = lax.axis_size("expert")
    split_count = lax.axis_size("etp")
    ring = split_count // 2
    me = lax.axis_index("etp")
    my_z = me // 2
    my_core = me % 2
    token_count, features = tokens.shape
    capacity = token_count // 4
    per_split = capacity // split_count
    pair_count = token_count * TOP

    flat_routes = routes.reshape(pair_count)
    expert_hot = (flat_routes[:, None] == jnp.arange(expert_count, dtype=jnp.int32)[None, :]).astype(
        jnp.int32
    )
    before = jnp.cumsum(expert_hot, axis=0) - expert_hot
    slots = jnp.sum(before * expert_hot, axis=1)

    mine = (slots // per_split) == me
    local_place = jnp.where(mine, flat_routes * per_split + slots % per_split, -1)
    place_count = expert_count * per_split
    pick = local_place[None, :] == jnp.arange(place_count, dtype=jnp.int32)[:, None]
    pick_tokens = jnp.any(pick.reshape(place_count, token_count, TOP), axis=2)

    scaled_grad = (combine_weights[:, :, None] * out_grad.astype(jnp.float32)[:, None, :]).astype(
        jnp.bfloat16
    )
    send_rows = select_rows(pick_tokens, tokens).astype(jnp.bfloat16)
    send_grad = select_rows(pick, scaled_grad.reshape(pair_count, features)).astype(jnp.bfloat16)
    send = jnp.concatenate(
        [
            send_rows.reshape(expert_count, per_split, features),
            send_grad.reshape(expert_count, per_split, features),
        ],
        axis=1,
    )
    recv = lax.all_to_all(send, "expert", split_axis=0, concat_axis=0, tiled=True)
    recv = recv.reshape(expert_count, 2, per_split, features).transpose(1, 0, 2, 3)
    gathered = etp_gather(recv.reshape(2, place_count, features), split_count)
    row_total = split_count * place_count
    rows_in = gathered[0].reshape(row_total, features)
    rows_grad = gathered[1].reshape(row_total, features)

    out_part, input_part, gate_weight_grad, up_weight_grad, down_weight_grad = expert_pass(
        rows_in, rows_grad, w_gate[0], w_up[0], w_down[0]
    )
    block = (split_count, 1, place_count, features)
    sums = etp_reduce(
        jnp.concatenate(
            [
                out_part.astype(jnp.bfloat16).astype(jnp.float32).reshape(block),
                input_part.astype(jnp.bfloat16).astype(jnp.float32).reshape(block),
            ],
            axis=1,
        ),
        split_count,
    ).astype(jnp.bfloat16)
    back = jnp.concatenate(
        [
            sums[0].reshape(expert_count, per_split, features),
            sums[1].reshape(expert_count, per_split, features),
        ],
        axis=1,
    )
    back = lax.all_to_all(back, "expert", split_axis=0, concat_axis=0, tiled=True)
    back = back.reshape(expert_count, 2, per_split, features).transpose(1, 0, 2, 3)
    tables = etp_gather(back.reshape(2, place_count, features), split_count)
    out_table = tables[0].reshape(row_total, features)
    input_table = tables[1].reshape(row_total, features)

    source = slots // per_split
    step = 2 * my_core - 1
    ring_offset = ((source // 2 - my_z) * step) % ring
    slot_of = jnp.array(SLOT_OF, dtype=jnp.int32)[ring_offset, (source % 2) ^ my_core]
    table_row = (slot_of * expert_count + flat_routes) * per_split + slots % per_split
    gather = table_row[:, None] == jnp.arange(row_total, dtype=jnp.int32)[None, :]
    out_pairs = select_rows(gather, out_table).reshape(token_count, TOP, features)
    input_pairs = select_rows(gather, input_table).reshape(token_count, TOP, features)
    grad_values = out_grad.astype(jnp.float32)
    mixed = jnp.sum(combine_weights[:, :, None] * out_pairs, axis=1).astype(jnp.bfloat16)
    combine_grad = jnp.sum(grad_values[:, None, :] * out_pairs, axis=2)
    tokens_grad = jnp.sum(input_pairs, axis=1).astype(jnp.bfloat16)
    return (
        mixed,
        tokens_grad,
        combine_grad,
        gate_weight_grad[None],
        up_weight_grad[None],
        down_weight_grad[None],
    )


def solution(mesh):
    return jax.shard_map(
        shards,
        mesh=mesh,
        in_specs=(
            P("expert", None),
            P("expert", None),
            P("expert", None),
            P("expert", None),
            P("expert", None, "etp"),
            P("expert", None, "etp"),
            P("expert", "etp", None),
        ),
        out_specs=(
            P("expert", None),
            P("expert", None),
            P("expert", None),
            P("expert", None, "etp"),
            P("expert", None, "etp"),
            P("expert", "etp", None),
        ),
        check_vma=False,
    )
```

```python
import jax
import jax.numpy as jnp
from jax import lax
from jax.sharding import PartitionSpec as P

TOP = 2


def contract_last(left, right):
    return lax.dot_general(
        left, right, (((1,), (1,)), ((), ())), preferred_element_type=jnp.float32
    )


def contract_first(left, right):
    return lax.dot_general(
        left, right, (((0,), (0,)), ((), ())), preferred_element_type=jnp.float32
    )


def select_rows(selector, table):
    return jnp.dot(selector.astype(table.dtype), table, preferred_element_type=jnp.float32)


def expert_pass(rows_in, rows_grad, gate_w, up_w, down_w):
    gate_pre = jnp.dot(rows_in, gate_w, preferred_element_type=jnp.float32)
    up_pre = jnp.dot(rows_in, up_w, preferred_element_type=jnp.float32)
    gate_sig = jax.nn.sigmoid(gate_pre)
    swish = gate_pre * gate_sig
    hidden = (swish * up_pre).astype(jnp.bfloat16)
    out_part = jnp.dot(hidden, down_w, preferred_element_type=jnp.float32)
    hidden_grad = contract_last(rows_grad, down_w)
    down_grad = contract_first(hidden, rows_grad).astype(jnp.bfloat16)
    gate_grad = (hidden_grad * up_pre * gate_sig * (1.0 + gate_pre * (1.0 - gate_sig))).astype(
        jnp.bfloat16
    )
    up_grad = (hidden_grad * swish).astype(jnp.bfloat16)
    gate_weight_grad = contract_first(rows_in, gate_grad).astype(jnp.bfloat16)
    up_weight_grad = contract_first(rows_in, up_grad).astype(jnp.bfloat16)
    input_part = contract_last(gate_grad, gate_w) + contract_last(up_grad, up_w)
    return (out_part, input_part, gate_weight_grad, up_weight_grad, down_grad)


def etp_perms(split_count):
    ring = split_count // 2
    swap = [(i, i ^ 1) for i in range(split_count)]
    onward = [(i, ((i // 2 + 1 - 2 * (i % 2)) % ring) * 2 + i % 2) for i in range(split_count)]
    backward = [(target, source) for source, target in onward]
    return swap, onward, backward


def etp_gather(unit, split_count, cover=None):
    swap, onward, _ = etp_perms(split_count)
    chip = jnp.stack([unit, lax.ppermute(unit, "etp", swap)], axis=1)
    first = lax.ppermute(chip, "etp", onward)
    if cover is not None:
        first, cover = lax.optimization_barrier((first, cover))
    second = lax.ppermute(first[:, 0], "etp", onward)
    held = jnp.concatenate([first, second[:, None]], axis=1)
    other = lax.ppermute(held, "etp", swap)
    return jnp.concatenate([chip, held, other], axis=1), cover


def etp_reduce(part, split_count):
    swap, _, backward = etp_perms(split_count)

    def send(value, perm):
        return lax.ppermute(value.astype(jnp.bfloat16), "etp", perm).astype(jnp.float32)

    held = part[2:5] + send(part[5:8], swap)
    near = held[0] + send(held[2], backward)
    chip = part[0:2] + send(jnp.stack([near, held[1]], axis=0), backward)
    return chip[0] + send(chip[1], swap)


def shards(tokens, out_grad, routes, combine_weights, w_gate, w_up, w_down):
    expert_count = lax.axis_size("expert")
    split_count = lax.axis_size("etp")
    ring = split_count // 2
    me = lax.axis_index("etp")
    my_z = me // 2
    my_core = me % 2
    token_count, features = tokens.shape
    capacity = token_count // 4
    per_split = capacity // split_count
    pair_count = token_count * TOP

    flat_routes = routes.reshape(pair_count)
    expert_hot = (flat_routes[:, None] == jnp.arange(expert_count, dtype=jnp.int32)[None, :]).astype(
        jnp.int32
    )
    before = jnp.cumsum(expert_hot, axis=0) - expert_hot
    slots = jnp.sum(before * expert_hot, axis=1)

    mine = (slots // per_split) == me
    local_place = jnp.where(mine, flat_routes * per_split + slots % per_split, -1)
    place_count = expert_count * per_split
    pick = local_place[None, :] == jnp.arange(place_count, dtype=jnp.int32)[:, None]
    pick_tokens = jnp.any(pick.reshape(place_count, token_count, TOP), axis=2)

    send_rows = select_rows(pick_tokens, tokens).astype(jnp.bfloat16)
    place_weight = jnp.sum(jnp.where(pick, combine_weights.reshape(1, pair_count), 0.0), axis=1)
    send_grad = (place_weight[:, None] * select_rows(pick_tokens, out_grad)).astype(jnp.bfloat16)
    send = jnp.concatenate(
        [
            send_rows.reshape(expert_count, per_split, features),
            send_grad.reshape(expert_count, per_split, features),
        ],
        axis=1,
    )
    recv = lax.all_to_all(send, "expert", split_axis=0, concat_axis=0, tiled=True)
    recv = recv.reshape(expert_count, 2, per_split, features).transpose(1, 0, 2, 3)
    gathered, _ = etp_gather(recv.reshape(2, place_count, features), split_count)
    row_total = split_count * place_count
    rows_in = gathered[0].reshape(row_total, features)
    rows_grad = gathered[1].reshape(row_total, features)

    out_part, input_part, gate_weight_grad, up_weight_grad, down_weight_grad = expert_pass(
        rows_in, rows_grad, w_gate[0], w_up[0], w_down[0]
    )
    block = (split_count, 1, place_count, features)
    sums = etp_reduce(
        jnp.concatenate(
            [
                out_part.astype(jnp.bfloat16).astype(jnp.float32).reshape(block),
                input_part.astype(jnp.bfloat16).astype(jnp.float32).reshape(block),
            ],
            axis=1,
        ),
        split_count,
    ).astype(jnp.bfloat16)
    back = jnp.concatenate(
        [
            sums[0].reshape(expert_count, per_split, features),
            sums[1].reshape(expert_count, per_split, features),
        ],
        axis=1,
    )
    back = lax.all_to_all(back, "expert", split_axis=0, concat_axis=0, tiled=True)
    back = back.reshape(expert_count, 2, per_split, features).transpose(1, 0, 2, 3)
    tables, weight_grads = etp_gather(
        back.reshape(2, place_count, features),
        split_count,
        (gate_weight_grad, up_weight_grad, down_weight_grad),
    )
    gate_weight_grad, up_weight_grad, down_weight_grad = weight_grads
    out_table = tables[0].reshape(row_total, features)
    input_table = tables[1].reshape(row_total, features)

    source = slots // per_split
    step = 2 * my_core - 1
    ring_offset = ((source // 2 - my_z) * step) % ring
    other_core = (source % 2) ^ my_core
    slot_of = jnp.where(
        ring_offset == 0,
        other_core,
        jnp.where(
            ring_offset == 1,
            2 + other_core,
            jnp.where(ring_offset == 2, 4 + 3 * other_core, 6 - other_core),
        ),
    )
    table_row = (slot_of * expert_count + flat_routes) * per_split + slots % per_split
    gather = table_row[:, None] == jnp.arange(row_total, dtype=jnp.int32)[None, :]
    out_pairs = select_rows(gather, out_table).reshape(token_count, TOP, features)
    input_pairs = select_rows(gather, input_table).reshape(token_count, TOP, features)
    grad_values = out_grad.astype(jnp.float32)
    mixed = jnp.sum(combine_weights[:, :, None] * out_pairs, axis=1).astype(jnp.bfloat16)
    combine_grad = jnp.sum(grad_values[:, None, :] * out_pairs, axis=2)
    tokens_grad = jnp.sum(input_pairs, axis=1).astype(jnp.bfloat16)
    return (
        mixed,
        tokens_grad,
        combine_grad,
        gate_weight_grad[None],
        up_weight_grad[None],
        down_weight_grad[None],
    )


def solution(mesh):
    return jax.shard_map(
        shards,
        mesh=mesh,
        in_specs=(
            P("expert", None),
            P("expert", None),
            P("expert", None),
            P("expert", None),
            P("expert", None, "etp"),
            P("expert", None, "etp"),
            P("expert", "etp", None),
        ),
        out_specs=(
            P("expert", None),
            P("expert", None),
            P("expert", None),
            P("expert", None, "etp"),
            P("expert", None, "etp"),
            P("expert", "etp", None),
        ),
        check_vma=False,
    )
```

```python
import jax
import jax.numpy as jnp
from jax import lax
from jax.sharding import PartitionSpec as P

TOP = 2


def contract_last(left, right):
    return lax.dot_general(
        left, right, (((1,), (1,)), ((), ())), preferred_element_type=jnp.float32
    )


def contract_first(left, right):
    return lax.dot_general(
        left, right, (((0,), (0,)), ((), ())), preferred_element_type=jnp.float32
    )


def select_rows(selector, table):
    return jnp.dot(selector.astype(table.dtype), table, preferred_element_type=jnp.float32)


def expert_rows(rows_in, rows_grad, gate_w, up_w, down_w):
    gate_pre = jnp.dot(rows_in, gate_w, preferred_element_type=jnp.float32)
    up_pre = jnp.dot(rows_in, up_w, preferred_element_type=jnp.float32)
    gate_sig = jax.nn.sigmoid(gate_pre)
    swish = gate_pre * gate_sig
    hidden = (swish * up_pre).astype(jnp.bfloat16)
    out_part = jnp.dot(hidden, down_w, preferred_element_type=jnp.float32)
    hidden_grad = contract_last(rows_grad, down_w)
    gate_grad = (hidden_grad * up_pre * gate_sig * (1.0 + gate_pre * (1.0 - gate_sig))).astype(
        jnp.bfloat16
    )
    up_grad = (hidden_grad * swish).astype(jnp.bfloat16)
    input_part = contract_last(gate_grad, gate_w) + contract_last(up_grad, up_w)
    return out_part, input_part, hidden, gate_grad, up_grad


def etp_perms(split_count):
    ring = split_count // 2
    swap = [(i, i ^ 1) for i in range(split_count)]
    onward = [(i, ((i // 2 + 1 - 2 * (i % 2)) % ring) * 2 + i % 2) for i in range(split_count)]
    backward = [(target, source) for source, target in onward]
    return swap, onward, backward


def etp_gather(unit, split_count, cover=None):
    swap, onward, _ = etp_perms(split_count)
    chip = jnp.stack([unit, lax.ppermute(unit, "etp", swap)], axis=1)
    first = lax.ppermute(chip, "etp", onward)
    if cover is not None:
        first, cover = lax.optimization_barrier((first, cover))
    second = lax.ppermute(first[:, 0], "etp", onward)
    held = jnp.concatenate([first, second[:, None]], axis=1)
    other = lax.ppermute(held, "etp", swap)
    return jnp.concatenate([chip, held, other], axis=1), cover


def etp_reduce(part, split_count):
    swap, _, backward = etp_perms(split_count)

    def send(value, perm):
        return lax.ppermute(value.astype(jnp.bfloat16), "etp", perm).astype(jnp.float32)

    held = part[2:5] + send(part[5:8], swap)
    near = held[0] + send(held[2], backward)
    chip = part[0:2] + send(jnp.stack([near, held[1]], axis=0), backward)
    return chip[0] + send(chip[1], swap)


def shards(tokens, out_grad, routes, combine_weights, w_gate, w_up, w_down):
    expert_count = lax.axis_size("expert")
    split_count = lax.axis_size("etp")
    ring = split_count // 2
    me = lax.axis_index("etp")
    my_z = me // 2
    my_core = me % 2
    token_count, features = tokens.shape
    capacity = token_count // 4
    per_split = capacity // split_count
    pair_count = token_count * TOP

    flat_routes = routes.reshape(pair_count)
    expert_hot = (flat_routes[:, None] == jnp.arange(expert_count, dtype=jnp.int32)[None, :]).astype(
        jnp.int32
    )
    before = jnp.cumsum(expert_hot, axis=0) - expert_hot
    slots = jnp.sum(before * expert_hot, axis=1)

    mine = (slots // per_split) == me
    local_place = jnp.where(mine, flat_routes * per_split + slots % per_split, -1)
    place_count = expert_count * per_split
    pick = local_place[None, :] == jnp.arange(place_count, dtype=jnp.int32)[:, None]
    pick_tokens = jnp.any(pick.reshape(place_count, token_count, TOP), axis=2)

    send_rows = select_rows(pick_tokens, tokens).astype(jnp.bfloat16)
    place_weight = jnp.sum(jnp.where(pick, combine_weights.reshape(1, pair_count), 0.0), axis=1)
    send_grad = (place_weight[:, None] * select_rows(pick_tokens, out_grad)).astype(jnp.bfloat16)
    send = jnp.concatenate(
        [
            send_rows.reshape(expert_count, per_split, features),
            send_grad.reshape(expert_count, per_split, features),
        ],
        axis=1,
    )
    recv = lax.all_to_all(send, "expert", split_axis=0, concat_axis=0, tiled=True)
    recv = recv.reshape(expert_count, 2, per_split, features).transpose(1, 0, 2, 3)
    unit = recv.reshape(2, place_count, features)

    swap, onward, _ = etp_perms(split_count)
    weights = (w_gate[0], w_up[0], w_down[0])
    chip = jnp.stack([unit, lax.ppermute(unit, "etp", swap)], axis=1)
    first = lax.ppermute(chip, "etp", onward)
    pieces = [chip.reshape(2, 2 * place_count, features)]
    results = [expert_rows(pieces[0][0], pieces[0][1], *weights)]
    first, results[0] = lax.optimization_barrier((first, results[0]))
    second = lax.ppermute(first[:, 0], "etp", onward)
    pieces.append(first.reshape(2, 2 * place_count, features))
    results.append(expert_rows(pieces[1][0], pieces[1][1], *weights))
    second, results[1] = lax.optimization_barrier((second, results[1]))
    held = jnp.concatenate([first, second[:, None]], axis=1)
    other = lax.ppermute(held, "etp", swap)
    pieces.append(jnp.concatenate([second[:, None], other], axis=1).reshape(2, 4 * place_count, features))
    results.append(expert_rows(pieces[2][0], pieces[2][1], *weights))

    rows_in = jnp.concatenate([piece[0] for piece in pieces], axis=0)
    rows_grad = jnp.concatenate([piece[1] for piece in pieces], axis=0)
    out_part, input_part, hidden, gate_grad, up_grad = (
        jnp.concatenate(parts, axis=0) for parts in zip(*results)
    )
    down_weight_grad = contract_first(hidden, rows_grad).astype(jnp.bfloat16)
    gate_weight_grad = contract_first(rows_in, gate_grad).astype(jnp.bfloat16)
    up_weight_grad = contract_first(rows_in, up_grad).astype(jnp.bfloat16)
    row_total = split_count * place_count

    block = (split_count, 1, place_count, features)
    sums = etp_reduce(
        jnp.concatenate(
            [
                out_part.astype(jnp.bfloat16).astype(jnp.float32).reshape(block),
                input_part.astype(jnp.bfloat16).astype(jnp.float32).reshape(block),
            ],
            axis=1,
        ),
        split_count,
    ).astype(jnp.bfloat16)
    back = jnp.concatenate(
        [
            sums[0].reshape(expert_count, per_split, features),
            sums[1].reshape(expert_count, per_split, features),
        ],
        axis=1,
    )
    back = lax.all_to_all(back, "expert", split_axis=0, concat_axis=0, tiled=True)
    back = back.reshape(expert_count, 2, per_split, features).transpose(1, 0, 2, 3)
    tables, weight_grads = etp_gather(
        back.reshape(2, place_count, features),
        split_count,
        (gate_weight_grad, up_weight_grad, down_weight_grad),
    )
    gate_weight_grad, up_weight_grad, down_weight_grad = weight_grads
    out_table = tables[0].reshape(row_total, features)
    input_table = tables[1].reshape(row_total, features)

    source = slots // per_split
    step = 2 * my_core - 1
    ring_offset = ((source // 2 - my_z) * step) % ring
    other_core = (source % 2) ^ my_core
    slot_of = jnp.where(
        ring_offset == 0,
        other_core,
        jnp.where(
            ring_offset == 1,
            2 + other_core,
            jnp.where(ring_offset == 2, 4 + 3 * other_core, 6 - other_core),
        ),
    )
    table_row = (slot_of * expert_count + flat_routes) * per_split + slots % per_split
    gather = table_row[:, None] == jnp.arange(row_total, dtype=jnp.int32)[None, :]
    out_pairs = select_rows(gather, out_table).reshape(token_count, TOP, features)
    input_pairs = select_rows(gather, input_table).reshape(token_count, TOP, features)
    grad_values = out_grad.astype(jnp.float32)
    mixed = jnp.sum(combine_weights[:, :, None] * out_pairs, axis=1).astype(jnp.bfloat16)
    combine_grad = jnp.sum(grad_values[:, None, :] * out_pairs, axis=2)
    tokens_grad = jnp.sum(input_pairs, axis=1).astype(jnp.bfloat16)
    return (
        mixed,
        tokens_grad,
        combine_grad,
        gate_weight_grad[None],
        up_weight_grad[None],
        down_weight_grad[None],
    )


def solution(mesh):
    return jax.shard_map(
        shards,
        mesh=mesh,
        in_specs=(
            P("expert", None),
            P("expert", None),
            P("expert", None),
            P("expert", None),
            P("expert", None, "etp"),
            P("expert", None, "etp"),
            P("expert", "etp", None),
        ),
        out_specs=(
            P("expert", None),
            P("expert", None),
            P("expert", None),
            P("expert", None, "etp"),
            P("expert", None, "etp"),
            P("expert", "etp", None),
        ),
        check_vma=False,
    )
```

```python
import jax
import jax.numpy as jnp
from jax import lax
from jax.sharding import PartitionSpec as P

TOP = 2


def contract_last(left, right):
    return lax.dot_general(
        left, right, (((1,), (1,)), ((), ())), preferred_element_type=jnp.float32
    )


def contract_first(left, right):
    return lax.dot_general(
        left, right, (((0,), (0,)), ((), ())), preferred_element_type=jnp.float32
    )


def select_rows(selector, table):
    return jnp.dot(selector.astype(table.dtype), table, preferred_element_type=jnp.float32)


def expert_rows(rows_in, rows_grad, gate_w, up_w, down_w):
    gate_pre = jnp.dot(rows_in, gate_w, preferred_element_type=jnp.float32)
    up_pre = jnp.dot(rows_in, up_w, preferred_element_type=jnp.float32)
    gate_sig = jax.nn.sigmoid(gate_pre)
    swish = gate_pre * gate_sig
    hidden = (swish * up_pre).astype(jnp.bfloat16)
    out_part = jnp.dot(hidden, down_w, preferred_element_type=jnp.float32)
    hidden_grad = contract_last(rows_grad, down_w)
    gate_grad = (hidden_grad * up_pre * gate_sig * (1.0 + gate_pre * (1.0 - gate_sig))).astype(
        jnp.bfloat16
    )
    up_grad = (hidden_grad * swish).astype(jnp.bfloat16)
    input_part = contract_last(gate_grad, gate_w) + contract_last(up_grad, up_w)
    return out_part, input_part, hidden, gate_grad, up_grad


def etp_perms(split_count):
    ring = split_count // 2
    swap = [(i, i ^ 1) for i in range(split_count)]
    onward = [(i, ((i // 2 + 1 - 2 * (i % 2)) % ring) * 2 + i % 2) for i in range(split_count)]
    backward = [(target, source) for source, target in onward]
    return swap, onward, backward


def etp_gather(unit, split_count, cover=None):
    swap, onward, _ = etp_perms(split_count)
    chip = jnp.stack([unit, lax.ppermute(unit, "etp", swap)], axis=1)
    first = lax.ppermute(chip, "etp", onward)
    if cover is not None:
        first, cover = lax.optimization_barrier((first, cover))
    second = lax.ppermute(first[:, 0], "etp", onward)
    held = jnp.concatenate([first, second[:, None]], axis=1)
    other = lax.ppermute(held, "etp", swap)
    return jnp.concatenate([chip, held, other], axis=1), cover


def etp_reduce(part, split_count, cover_near=None, cover_far=None):
    swap, _, backward = etp_perms(split_count)

    def send(value, perm):
        return lax.ppermute(value.astype(jnp.bfloat16), "etp", perm).astype(jnp.float32)

    held = part[2:5] + send(part[5:8], swap)
    arrived = send(held[2], backward)
    arrived, cover_near = lax.optimization_barrier((arrived, cover_near))
    near = held[0] + arrived
    arrived = send(jnp.stack([near, held[1]], axis=0), backward)
    arrived, cover_far = lax.optimization_barrier((arrived, cover_far))
    chip = part[0:2] + arrived
    return chip[0] + send(chip[1], swap), cover_near, cover_far


def shards(tokens, out_grad, routes, combine_weights, w_gate, w_up, w_down):
    expert_count = lax.axis_size("expert")
    split_count = lax.axis_size("etp")
    ring = split_count // 2
    me = lax.axis_index("etp")
    my_z = me // 2
    my_core = me % 2
    token_count, features = tokens.shape
    capacity = token_count // 4
    per_split = capacity // split_count
    pair_count = token_count * TOP

    flat_routes = routes.reshape(pair_count)
    expert_hot = (flat_routes[:, None] == jnp.arange(expert_count, dtype=jnp.int32)[None, :]).astype(
        jnp.int32
    )
    before = jnp.cumsum(expert_hot, axis=0) - expert_hot
    slots = jnp.sum(before * expert_hot, axis=1)

    mine = (slots // per_split) == me
    local_place = jnp.where(mine, flat_routes * per_split + slots % per_split, -1)
    place_count = expert_count * per_split
    pick = local_place[None, :] == jnp.arange(place_count, dtype=jnp.int32)[:, None]
    pick_tokens = jnp.any(pick.reshape(place_count, token_count, TOP), axis=2)

    send_rows = select_rows(pick_tokens, tokens).astype(jnp.bfloat16)
    place_weight = jnp.sum(jnp.where(pick, combine_weights.reshape(1, pair_count), 0.0), axis=1)
    send_grad = (place_weight[:, None] * select_rows(pick_tokens, out_grad)).astype(jnp.bfloat16)
    send = jnp.concatenate(
        [
            send_rows.reshape(expert_count, per_split, features),
            send_grad.reshape(expert_count, per_split, features),
        ],
        axis=1,
    )
    recv = lax.all_to_all(send, "expert", split_axis=0, concat_axis=0, tiled=True)
    recv = recv.reshape(expert_count, 2, per_split, features).transpose(1, 0, 2, 3)
    unit = recv.reshape(2, place_count, features)

    swap, onward, _ = etp_perms(split_count)
    weights = (w_gate[0], w_up[0], w_down[0])
    chip = jnp.stack([unit, lax.ppermute(unit, "etp", swap)], axis=1)
    first = lax.ppermute(chip, "etp", onward)
    pieces = [chip.reshape(2, 2 * place_count, features)]
    results = [expert_rows(pieces[0][0], pieces[0][1], *weights)]
    first, results[0] = lax.optimization_barrier((first, results[0]))
    second = lax.ppermute(first[:, 0], "etp", onward)
    pieces.append(first.reshape(2, 2 * place_count, features))
    results.append(expert_rows(pieces[1][0], pieces[1][1], *weights))
    second, results[1] = lax.optimization_barrier((second, results[1]))
    held = jnp.concatenate([first, second[:, None]], axis=1)
    other = lax.ppermute(held, "etp", swap)
    pieces.append(jnp.concatenate([second[:, None], other], axis=1).reshape(2, 4 * place_count, features))
    results.append(expert_rows(pieces[2][0], pieces[2][1], *weights))

    rows_in = jnp.concatenate([piece[0] for piece in pieces], axis=0)
    rows_grad = jnp.concatenate([piece[1] for piece in pieces], axis=0)
    out_part, input_part, hidden, gate_grad, up_grad = (
        jnp.concatenate(parts, axis=0) for parts in zip(*results)
    )
    row_total = split_count * place_count

    block = (split_count, 1, place_count, features)
    sums, down_weight_grad, (gate_weight_grad, up_weight_grad) = etp_reduce(
        jnp.concatenate(
            [
                out_part.astype(jnp.bfloat16).astype(jnp.float32).reshape(block),
                input_part.astype(jnp.bfloat16).astype(jnp.float32).reshape(block),
            ],
            axis=1,
        ),
        split_count,
        contract_first(hidden, rows_grad).astype(jnp.bfloat16),
        (
            contract_first(rows_in, gate_grad).astype(jnp.bfloat16),
            contract_first(rows_in, up_grad).astype(jnp.bfloat16),
        ),
    )
    sums = sums.astype(jnp.bfloat16)
    back = jnp.concatenate(
        [
            sums[0].reshape(expert_count, per_split, features),
            sums[1].reshape(expert_count, per_split, features),
        ],
        axis=1,
    )
    back = lax.all_to_all(back, "expert", split_axis=0, concat_axis=0, tiled=True)
    back = back.reshape(expert_count, 2, per_split, features).transpose(1, 0, 2, 3)
    tables, _ = etp_gather(back.reshape(2, place_count, features), split_count)
    out_table = tables[0].reshape(row_total, features)
    input_table = tables[1].reshape(row_total, features)

    source = slots // per_split
    step = 2 * my_core - 1
    ring_offset = ((source // 2 - my_z) * step) % ring
    other_core = (source % 2) ^ my_core
    slot_of = jnp.where(
        ring_offset == 0,
        other_core,
        jnp.where(
            ring_offset == 1,
            2 + other_core,
            jnp.where(ring_offset == 2, 4 + 3 * other_core, 6 - other_core),
        ),
    )
    table_row = (slot_of * expert_count + flat_routes) * per_split + slots % per_split
    gather = table_row[:, None] == jnp.arange(row_total, dtype=jnp.int32)[None, :]
    out_pairs = select_rows(gather, out_table).reshape(token_count, TOP, features)
    input_pairs = select_rows(gather, input_table).reshape(token_count, TOP, features)
    grad_values = out_grad.astype(jnp.float32)
    mixed = jnp.sum(combine_weights[:, :, None] * out_pairs, axis=1).astype(jnp.bfloat16)
    combine_grad = jnp.sum(grad_values[:, None, :] * out_pairs, axis=2)
    tokens_grad = jnp.sum(input_pairs, axis=1).astype(jnp.bfloat16)
    return (
        mixed,
        tokens_grad,
        combine_grad,
        gate_weight_grad[None],
        up_weight_grad[None],
        down_weight_grad[None],
    )


def solution(mesh):
    return jax.shard_map(
        shards,
        mesh=mesh,
        in_specs=(
            P("expert", None),
            P("expert", None),
            P("expert", None),
            P("expert", None),
            P("expert", None, "etp"),
            P("expert", None, "etp"),
            P("expert", "etp", None),
        ),
        out_specs=(
            P("expert", None),
            P("expert", None),
            P("expert", None),
            P("expert", None, "etp"),
            P("expert", None, "etp"),
            P("expert", "etp", None),
        ),
        check_vma=False,
    )
```

```python
import jax
import jax.numpy as jnp
from jax import lax
from jax.sharding import PartitionSpec as P

TOP = 2


def contract_last(left, right):
    return lax.dot_general(
        left, right, (((1,), (1,)), ((), ())), preferred_element_type=jnp.float32
    )


def contract_first(left, right):
    return lax.dot_general(
        left, right, (((0,), (0,)), ((), ())), preferred_element_type=jnp.float32
    )


def select_rows(selector, table):
    return jnp.dot(selector.astype(table.dtype), table, preferred_element_type=jnp.float32)


def expert_rows(rows_in, rows_grad, gate_w, up_w, down_w):
    gate_pre = jnp.dot(rows_in, gate_w, preferred_element_type=jnp.float32)
    up_pre = jnp.dot(rows_in, up_w, preferred_element_type=jnp.float32)
    gate_sig = jax.nn.sigmoid(gate_pre)
    swish = gate_pre * gate_sig
    hidden = (swish * up_pre).astype(jnp.bfloat16)
    out_part = jnp.dot(hidden, down_w, preferred_element_type=jnp.float32)
    hidden_grad = contract_last(rows_grad, down_w)
    gate_grad = (hidden_grad * up_pre * gate_sig * (1.0 + gate_pre * (1.0 - gate_sig))).astype(
        jnp.bfloat16
    )
    up_grad = (hidden_grad * swish).astype(jnp.bfloat16)
    input_part = contract_last(gate_grad, gate_w) + contract_last(up_grad, up_w)
    return out_part, input_part, hidden, gate_grad, up_grad


def etp_perms(split_count):
    ring = split_count // 2
    swap = [(i, i ^ 1) for i in range(split_count)]
    onward = [(i, ((i // 2 + 1 - 2 * (i % 2)) % ring) * 2 + i % 2) for i in range(split_count)]
    backward = [(target, source) for source, target in onward]
    return swap, onward, backward


def etp_gather(unit, split_count, cover=None):
    swap, onward, _ = etp_perms(split_count)
    chip = jnp.stack([unit, lax.ppermute(unit, "etp", swap)], axis=1)
    first = lax.ppermute(chip, "etp", onward)
    if cover is not None:
        first, cover = lax.optimization_barrier((first, cover))
    second = lax.ppermute(first[:, 0], "etp", onward)
    held = jnp.concatenate([first, second[:, None]], axis=1)
    other = lax.ppermute(held, "etp", swap)
    return jnp.concatenate([chip, held, other], axis=1), cover


def etp_reduce(part, split_count, cover_near=None, cover_far=None):
    swap, _, backward = etp_perms(split_count)

    def send(value, perm):
        return lax.ppermute(value.astype(jnp.bfloat16), "etp", perm).astype(jnp.float32)

    held = part[2:5] + send(part[5:8], swap)
    arrived = send(held[2], backward)
    arrived, cover_near = lax.optimization_barrier((arrived, cover_near))
    near = held[0] + arrived
    arrived = send(jnp.stack([near, held[1]], axis=0), backward)
    arrived, cover_far = lax.optimization_barrier((arrived, cover_far))
    chip = part[0:2] + arrived
    return chip[0] + send(chip[1], swap), cover_near, cover_far


def shards(tokens, out_grad, routes, combine_weights, w_gate, w_up, w_down):
    expert_count = lax.axis_size("expert")
    split_count = lax.axis_size("etp")
    ring = split_count // 2
    me = lax.axis_index("etp")
    my_z = me // 2
    my_core = me % 2
    token_count, features = tokens.shape
    capacity = token_count // 4
    per_split = capacity // split_count
    pair_count = token_count * TOP

    flat_routes = routes.reshape(pair_count)
    expert_hot = (flat_routes[:, None] == jnp.arange(expert_count, dtype=jnp.int32)[None, :]).astype(
        jnp.int32
    )
    before = jnp.cumsum(expert_hot, axis=0) - expert_hot
    slots = jnp.sum(before * expert_hot, axis=1)

    mine = (slots // per_split) == me
    local_place = jnp.where(mine, flat_routes * per_split + slots % per_split, -1)
    place_count = expert_count * per_split
    pick = local_place[None, :] == jnp.arange(place_count, dtype=jnp.int32)[:, None]
    pick_tokens = jnp.any(pick.reshape(place_count, token_count, TOP), axis=2)

    send_rows = select_rows(pick_tokens, tokens).astype(jnp.bfloat16)
    place_weight = jnp.sum(jnp.where(pick, combine_weights.reshape(1, pair_count), 0.0), axis=1)
    send_grad = (place_weight[:, None] * select_rows(pick_tokens, out_grad)).astype(jnp.bfloat16)
    send = jnp.concatenate([send_rows, send_grad], axis=1).reshape(
        expert_count, per_split, 2 * features
    )
    recv = lax.all_to_all(send, "expert", split_axis=0, concat_axis=0, tiled=True)
    unit = recv.reshape(place_count, 2 * features)

    swap, onward, _ = etp_perms(split_count)
    weights = (w_gate[0], w_up[0], w_down[0])
    chip = jnp.stack([unit, lax.ppermute(unit, "etp", swap)], axis=0)
    first = lax.ppermute(chip, "etp", onward)
    pieces = [chip.reshape(2 * place_count, 2 * features)]
    results = [expert_rows(pieces[0][:, :features], pieces[0][:, features:], *weights)]
    first, results[0] = lax.optimization_barrier((first, results[0]))
    second = lax.ppermute(first[0], "etp", onward)
    pieces.append(first.reshape(2 * place_count, 2 * features))
    results.append(expert_rows(pieces[1][:, :features], pieces[1][:, features:], *weights))
    second, results[1] = lax.optimization_barrier((second, results[1]))
    held = jnp.concatenate([first, second[None]], axis=0)
    other = lax.ppermute(held, "etp", swap)
    pieces.append(jnp.concatenate([second[None], other], axis=0).reshape(4 * place_count, 2 * features))
    results.append(expert_rows(pieces[2][:, :features], pieces[2][:, features:], *weights))

    rows_in = jnp.concatenate([piece[:, :features] for piece in pieces], axis=0)
    rows_grad = jnp.concatenate([piece[:, features:] for piece in pieces], axis=0)
    out_part, input_part, hidden, gate_grad, up_grad = (
        jnp.concatenate(parts, axis=0) for parts in zip(*results)
    )
    row_total = split_count * place_count

    block = (split_count, 1, place_count, features)
    sums, down_weight_grad, (gate_weight_grad, up_weight_grad) = etp_reduce(
        jnp.concatenate(
            [
                out_part.astype(jnp.bfloat16).astype(jnp.float32).reshape(block),
                input_part.astype(jnp.bfloat16).astype(jnp.float32).reshape(block),
            ],
            axis=1,
        ),
        split_count,
        contract_first(hidden, rows_grad).astype(jnp.bfloat16),
        (
            contract_first(rows_in, gate_grad).astype(jnp.bfloat16),
            contract_first(rows_in, up_grad).astype(jnp.bfloat16),
        ),
    )
    sums = sums.astype(jnp.bfloat16)
    back = jnp.concatenate(
        [
            sums[0].reshape(expert_count, per_split, features),
            sums[1].reshape(expert_count, per_split, features),
        ],
        axis=1,
    )
    back = lax.all_to_all(back, "expert", split_axis=0, concat_axis=0, tiled=True)
    back = back.reshape(expert_count, 2, per_split, features).transpose(1, 0, 2, 3)
    tables, _ = etp_gather(back.reshape(2, place_count, features), split_count)
    out_table = tables[0].reshape(row_total, features)
    input_table = tables[1].reshape(row_total, features)

    source = slots // per_split
    step = 2 * my_core - 1
    ring_offset = ((source // 2 - my_z) * step) % ring
    other_core = (source % 2) ^ my_core
    slot_of = jnp.where(
        ring_offset == 0,
        other_core,
        jnp.where(
            ring_offset == 1,
            2 + other_core,
            jnp.where(ring_offset == 2, 4 + 3 * other_core, 6 - other_core),
        ),
    )
    table_row = (slot_of * expert_count + flat_routes) * per_split + slots % per_split
    gather = table_row[:, None] == jnp.arange(row_total, dtype=jnp.int32)[None, :]
    out_pairs = select_rows(gather, out_table).reshape(token_count, TOP, features)
    input_pairs = select_rows(gather, input_table).reshape(token_count, TOP, features)
    grad_values = out_grad.astype(jnp.float32)
    mixed = jnp.sum(combine_weights[:, :, None] * out_pairs, axis=1).astype(jnp.bfloat16)
    combine_grad = jnp.sum(grad_values[:, None, :] * out_pairs, axis=2)
    tokens_grad = jnp.sum(input_pairs, axis=1).astype(jnp.bfloat16)
    return (
        mixed,
        tokens_grad,
        combine_grad,
        gate_weight_grad[None],
        up_weight_grad[None],
        down_weight_grad[None],
    )


def solution(mesh):
    return jax.shard_map(
        shards,
        mesh=mesh,
        in_specs=(
            P("expert", None),
            P("expert", None),
            P("expert", None),
            P("expert", None),
            P("expert", None, "etp"),
            P("expert", None, "etp"),
            P("expert", "etp", None),
        ),
        out_specs=(
            P("expert", None),
            P("expert", None),
            P("expert", None),
            P("expert", None, "etp"),
            P("expert", None, "etp"),
            P("expert", "etp", None),
        ),
        check_vma=False,
    )
```

```python
import jax
import jax.numpy as jnp
from jax import lax
from jax.sharding import PartitionSpec as P

TOP = 2


def contract_last(left, right):
    return lax.dot_general(
        left, right, (((1,), (1,)), ((), ())), preferred_element_type=jnp.float32
    )


def contract_first(left, right):
    return lax.dot_general(
        left, right, (((0,), (0,)), ((), ())), preferred_element_type=jnp.float32
    )


def select_rows(selector, table):
    return jnp.dot(selector.astype(table.dtype), table, preferred_element_type=jnp.float32)


def expert_rows(rows_in, rows_grad, gate_w, up_w, down_w):
    gate_pre = jnp.dot(rows_in, gate_w, preferred_element_type=jnp.float32)
    up_pre = jnp.dot(rows_in, up_w, preferred_element_type=jnp.float32)
    gate_sig = jax.nn.sigmoid(gate_pre)
    swish = gate_pre * gate_sig
    hidden = (swish * up_pre).astype(jnp.bfloat16)
    out_part = jnp.dot(hidden, down_w, preferred_element_type=jnp.float32)
    hidden_grad = contract_last(rows_grad, down_w)
    gate_grad = (hidden_grad * up_pre * gate_sig * (1.0 + gate_pre * (1.0 - gate_sig))).astype(
        jnp.bfloat16
    )
    up_grad = (hidden_grad * swish).astype(jnp.bfloat16)
    input_part = contract_last(gate_grad, gate_w) + contract_last(up_grad, up_w)
    return out_part, input_part, hidden, gate_grad, up_grad


def etp_perms(split_count):
    ring = split_count // 2
    swap = [(i, i ^ 1) for i in range(split_count)]
    onward = [(i, ((i // 2 + 1 - 2 * (i % 2)) % ring) * 2 + i % 2) for i in range(split_count)]
    backward = [(target, source) for source, target in onward]
    return swap, onward, backward


def etp_gather(unit, split_count, cover=None):
    swap, onward, _ = etp_perms(split_count)
    chip = jnp.stack([unit, lax.ppermute(unit, "etp", swap)], axis=1)
    first = lax.ppermute(chip, "etp", onward)
    if cover is not None:
        first, cover = lax.optimization_barrier((first, cover))
    second = lax.ppermute(first[:, 0], "etp", onward)
    held = jnp.concatenate([first, second[:, None]], axis=1)
    other = lax.ppermute(held, "etp", swap)
    return jnp.concatenate([chip, held, other], axis=1), cover


def etp_reduce(part, split_count, cover_near=None, cover_far=None):
    swap, _, backward = etp_perms(split_count)

    def send(value, perm):
        return lax.ppermute(value.astype(jnp.bfloat16), "etp", perm).astype(jnp.float32)

    held = part[2:5] + send(part[5:8], swap)
    arrived = send(held[2], backward)
    arrived, cover_near = lax.optimization_barrier((arrived, cover_near))
    near = held[0] + arrived
    arrived = send(jnp.stack([near, held[1]], axis=0), backward)
    arrived, cover_far = lax.optimization_barrier((arrived, cover_far))
    chip = part[0:2] + arrived
    return chip[0] + send(chip[1], swap), cover_near, cover_far


def shards(tokens, out_grad, routes, combine_weights, w_gate, w_up, w_down):
    expert_count = lax.axis_size("expert")
    split_count = lax.axis_size("etp")
    ring = split_count // 2
    me = lax.axis_index("etp")
    my_z = me // 2
    my_core = me % 2
    token_count, features = tokens.shape
    capacity = token_count // 4
    per_split = capacity // split_count
    pair_count = token_count * TOP

    flat_routes = routes.reshape(pair_count)
    expert_hot = (flat_routes[:, None] == jnp.arange(expert_count, dtype=jnp.int32)[None, :]).astype(
        jnp.int32
    )
    before = jnp.cumsum(expert_hot, axis=0) - expert_hot
    slots = jnp.sum(before * expert_hot, axis=1)

    mine = (slots // per_split) == me
    local_place = jnp.where(mine, flat_routes * per_split + slots % per_split, -1)
    place_count = expert_count * per_split
    pick = local_place[None, :] == jnp.arange(place_count, dtype=jnp.int32)[:, None]
    pick_tokens = jnp.any(pick.reshape(place_count, token_count, TOP), axis=2)

    send_rows = select_rows(pick_tokens, tokens).astype(jnp.bfloat16)
    place_weight = jnp.sum(jnp.where(pick, combine_weights.reshape(1, pair_count), 0.0), axis=1)
    send_grad = (place_weight[:, None] * select_rows(pick_tokens, out_grad)).astype(jnp.bfloat16)
    send = jnp.concatenate([send_rows, send_grad], axis=1).reshape(
        expert_count, per_split, 2 * features
    )
    recv = lax.all_to_all(send, "expert", split_axis=0, concat_axis=0, tiled=True)
    unit = recv.reshape(place_count, 2 * features)

    swap, onward, _ = etp_perms(split_count)
    weights = (w_gate[0], w_up[0], w_down[0])
    chip = jnp.stack([unit, lax.ppermute(unit, "etp", swap)], axis=0)
    first = lax.ppermute(chip, "etp", onward)
    pieces = [chip.reshape(2 * place_count, 2 * features)]
    results = [expert_rows(pieces[0][:, :features], pieces[0][:, features:], *weights)]
    first, results[0] = lax.optimization_barrier((first, results[0]))
    second = lax.ppermute(first[0], "etp", onward)
    first_other = lax.ppermute(first, "etp", swap)
    pieces.append(first.reshape(2 * place_count, 2 * features))
    results.append(expert_rows(pieces[1][:, :features], pieces[1][:, features:], *weights))
    pieces.append(first_other.reshape(2 * place_count, 2 * features))
    results.append(expert_rows(pieces[2][:, :features], pieces[2][:, features:], *weights))
    second, results[1], results[2] = lax.optimization_barrier((second, results[1], results[2]))
    second_other = lax.ppermute(second, "etp", swap)
    pieces.append(jnp.concatenate([second, second_other], axis=0))
    results.append(expert_rows(pieces[3][:, :features], pieces[3][:, features:], *weights))

    rows_in = jnp.concatenate([piece[:, :features] for piece in pieces], axis=0)
    rows_grad = jnp.concatenate([piece[:, features:] for piece in pieces], axis=0)
    hidden, gate_grad, up_grad = (
        jnp.concatenate(parts, axis=0) for parts in list(zip(*results))[2:]
    )
    out_part, input_part = (
        jnp.concatenate(
            [parts[0], parts[1], parts[3][:place_count], parts[2], parts[3][place_count:]], axis=0
        )
        for parts in list(zip(*results))[:2]
    )
    row_total = split_count * place_count

    block = (split_count, 1, place_count, features)
    sums, down_weight_grad, (gate_weight_grad, up_weight_grad) = etp_reduce(
        jnp.concatenate(
            [
                out_part.astype(jnp.bfloat16).astype(jnp.float32).reshape(block),
                input_part.astype(jnp.bfloat16).astype(jnp.float32).reshape(block),
            ],
            axis=1,
        ),
        split_count,
        contract_first(hidden, rows_grad).astype(jnp.bfloat16),
        (
            contract_first(rows_in, gate_grad).astype(jnp.bfloat16),
            contract_first(rows_in, up_grad).astype(jnp.bfloat16),
        ),
    )
    sums = sums.astype(jnp.bfloat16)
    back = jnp.concatenate(
        [
            sums[0].reshape(expert_count, per_split, features),
            sums[1].reshape(expert_count, per_split, features),
        ],
        axis=1,
    )
    back = lax.all_to_all(back, "expert", split_axis=0, concat_axis=0, tiled=True)
    back = back.reshape(expert_count, 2, per_split, features).transpose(1, 0, 2, 3)
    tables, _ = etp_gather(back.reshape(2, place_count, features), split_count)
    out_table = tables[0].reshape(row_total, features)
    input_table = tables[1].reshape(row_total, features)

    source = slots // per_split
    step = 2 * my_core - 1
    ring_offset = ((source // 2 - my_z) * step) % ring
    other_core = (source % 2) ^ my_core
    slot_of = jnp.where(
        ring_offset == 0,
        other_core,
        jnp.where(
            ring_offset == 1,
            2 + other_core,
            jnp.where(ring_offset == 2, 4 + 3 * other_core, 6 - other_core),
        ),
    )
    table_row = (slot_of * expert_count + flat_routes) * per_split + slots % per_split
    gather = table_row[:, None] == jnp.arange(row_total, dtype=jnp.int32)[None, :]
    out_pairs = select_rows(gather, out_table).reshape(token_count, TOP, features)
    input_pairs = select_rows(gather, input_table).reshape(token_count, TOP, features)
    grad_values = out_grad.astype(jnp.float32)
    mixed = jnp.sum(combine_weights[:, :, None] * out_pairs, axis=1).astype(jnp.bfloat16)
    combine_grad = jnp.sum(grad_values[:, None, :] * out_pairs, axis=2)
    tokens_grad = jnp.sum(input_pairs, axis=1).astype(jnp.bfloat16)
    return (
        mixed,
        tokens_grad,
        combine_grad,
        gate_weight_grad[None],
        up_weight_grad[None],
        down_weight_grad[None],
    )


def solution(mesh):
    return jax.shard_map(
        shards,
        mesh=mesh,
        in_specs=(
            P("expert", None),
            P("expert", None),
            P("expert", None),
            P("expert", None),
            P("expert", None, "etp"),
            P("expert", None, "etp"),
            P("expert", "etp", None),
        ),
        out_specs=(
            P("expert", None),
            P("expert", None),
            P("expert", None),
            P("expert", None, "etp"),
            P("expert", None, "etp"),
            P("expert", "etp", None),
        ),
        check_vma=False,
    )
```

```python
import jax
import jax.numpy as jnp
from jax import lax
from jax.sharding import PartitionSpec as P

TOP = 2


def contract_last(left, right):
    return lax.dot_general(
        left, right, (((1,), (1,)), ((), ())), preferred_element_type=jnp.float32
    )


def contract_first(left, right):
    return lax.dot_general(
        left, right, (((0,), (0,)), ((), ())), preferred_element_type=jnp.float32
    )


def select_rows(selector, table):
    return jnp.dot(selector.astype(table.dtype), table, preferred_element_type=jnp.float32)


def expert_rows(rows_in, rows_grad, gate_w, up_w, down_w):
    gate_pre = jnp.dot(rows_in, gate_w, preferred_element_type=jnp.float32)
    up_pre = jnp.dot(rows_in, up_w, preferred_element_type=jnp.float32)
    gate_sig = jax.nn.sigmoid(gate_pre)
    swish = gate_pre * gate_sig
    hidden = (swish * up_pre).astype(jnp.bfloat16)
    out_part = jnp.dot(hidden, down_w, preferred_element_type=jnp.float32)
    hidden_grad = contract_last(rows_grad, down_w)
    gate_grad = (hidden_grad * up_pre * gate_sig * (1.0 + gate_pre * (1.0 - gate_sig))).astype(
        jnp.bfloat16
    )
    up_grad = (hidden_grad * swish).astype(jnp.bfloat16)
    input_part = contract_last(gate_grad, gate_w) + contract_last(up_grad, up_w)
    return out_part, input_part, hidden, gate_grad, up_grad


def etp_perms(split_count):
    ring = split_count // 2
    swap = [(i, i ^ 1) for i in range(split_count)]
    onward = [(i, ((i // 2 + 1 - 2 * (i % 2)) % ring) * 2 + i % 2) for i in range(split_count)]
    backward = [(target, source) for source, target in onward]
    return swap, onward, backward


def etp_gather(unit, split_count, cover=None):
    swap, onward, _ = etp_perms(split_count)
    chip = jnp.stack([unit, lax.ppermute(unit, "etp", swap)], axis=1)
    first = lax.ppermute(chip, "etp", onward)
    if cover is not None:
        first, cover = lax.optimization_barrier((first, cover))
    second = lax.ppermute(first[:, 0], "etp", onward)
    held = jnp.concatenate([first, second[:, None]], axis=1)
    other = lax.ppermute(held, "etp", swap)
    return jnp.concatenate([chip, held, other], axis=1), cover


def etp_reduce(part, split_count, cover_near=None, cover_far=None):
    swap, _, backward = etp_perms(split_count)

    def send(value, perm):
        return lax.ppermute(value.astype(jnp.bfloat16), "etp", perm).astype(jnp.float32)

    held = part[2:5] + send(part[5:8], swap)
    arrived = send(held[2], backward)
    arrived, cover_near = lax.optimization_barrier((arrived, cover_near))
    near = held[0] + arrived
    arrived = send(jnp.stack([near, held[1]], axis=0), backward)
    arrived, cover_far = lax.optimization_barrier((arrived, cover_far))
    chip = part[0:2] + arrived
    return chip[0] + send(chip[1], swap), cover_near, cover_far


def shards(tokens, out_grad, routes, combine_weights, w_gate, w_up, w_down):
    expert_count = lax.axis_size("expert")
    split_count = lax.axis_size("etp")
    ring = split_count // 2
    me = lax.axis_index("etp")
    my_z = me // 2
    my_core = me % 2
    token_count, features = tokens.shape
    capacity = token_count // 4
    per_split = capacity // split_count
    pair_count = token_count * TOP

    flat_routes = routes.reshape(pair_count)
    expert_hot = (flat_routes[:, None] == jnp.arange(expert_count, dtype=jnp.int32)[None, :]).astype(
        jnp.int32
    )
    before = jnp.cumsum(expert_hot, axis=0) - expert_hot
    slots = jnp.sum(before * expert_hot, axis=1)

    mine = (slots // per_split) == me
    local_place = jnp.where(mine, flat_routes * per_split + slots % per_split, -1)
    place_count = expert_count * per_split
    pick = local_place[None, :] == jnp.arange(place_count, dtype=jnp.int32)[:, None]
    pick_tokens = jnp.any(pick.reshape(place_count, token_count, TOP), axis=2)

    send_rows = select_rows(pick_tokens, tokens).astype(jnp.bfloat16)
    place_weight = jnp.sum(jnp.where(pick, combine_weights.reshape(1, pair_count), 0.0), axis=1)
    send_grad = (place_weight[:, None] * select_rows(pick_tokens, out_grad)).astype(jnp.bfloat16)
    send = jnp.concatenate([send_rows, send_grad], axis=1).reshape(
        expert_count, per_split, 2 * features
    )
    recv = lax.all_to_all(send, "expert", split_axis=0, concat_axis=0, tiled=True)
    unit = recv.reshape(place_count, 2 * features)

    swap, onward, _ = etp_perms(split_count)
    weights = (w_gate[0], w_up[0], w_down[0])
    chip = jnp.stack([unit, lax.ppermute(unit, "etp", swap)], axis=0)
    first = lax.ppermute(chip, "etp", onward)
    pieces = [chip.reshape(2 * place_count, 2 * features)]
    results = [expert_rows(pieces[0][:, :features], pieces[0][:, features:], *weights)]
    first, results[0] = lax.optimization_barrier((first, results[0]))
    second = lax.ppermute(first[0], "etp", onward)
    first_other = lax.ppermute(first, "etp", swap)
    pieces.append(jnp.concatenate([first, first_other], axis=0).reshape(4 * place_count, 2 * features))
    results.append(expert_rows(pieces[1][:, :features], pieces[1][:, features:], *weights))
    second, results[1] = lax.optimization_barrier((second, results[1]))
    second_other = lax.ppermute(second, "etp", swap)
    pieces.append(jnp.concatenate([second, second_other], axis=0))
    results.append(expert_rows(pieces[2][:, :features], pieces[2][:, features:], *weights))

    rows_in = jnp.concatenate([piece[:, :features] for piece in pieces], axis=0)
    rows_grad = jnp.concatenate([piece[:, features:] for piece in pieces], axis=0)
    hidden, gate_grad, up_grad = (
        jnp.concatenate(parts, axis=0) for parts in list(zip(*results))[2:]
    )
    pair_rows = 2 * place_count
    out_part, input_part = (
        jnp.concatenate(
            [
                parts[0],
                parts[1][:pair_rows],
                parts[2][:place_count],
                parts[1][pair_rows:],
                parts[2][place_count:],
            ],
            axis=0,
        )
        for parts in list(zip(*results))[:2]
    )
    row_total = split_count * place_count

    block = (split_count, 1, place_count, features)
    sums, down_weight_grad, (gate_weight_grad, up_weight_grad) = etp_reduce(
        jnp.concatenate(
            [
                out_part.astype(jnp.bfloat16).astype(jnp.float32).reshape(block),
                input_part.astype(jnp.bfloat16).astype(jnp.float32).reshape(block),
            ],
            axis=1,
        ),
        split_count,
        contract_first(hidden, rows_grad).astype(jnp.bfloat16),
        (
            contract_first(rows_in, gate_grad).astype(jnp.bfloat16),
            contract_first(rows_in, up_grad).astype(jnp.bfloat16),
        ),
    )
    sums = sums.astype(jnp.bfloat16)
    back = jnp.concatenate(
        [
            sums[0].reshape(expert_count, per_split, features),
            sums[1].reshape(expert_count, per_split, features),
        ],
        axis=1,
    )
    back = lax.all_to_all(back, "expert", split_axis=0, concat_axis=0, tiled=True)
    back = back.reshape(expert_count, 2, per_split, features).transpose(1, 0, 2, 3)
    tables, _ = etp_gather(back.reshape(2, place_count, features), split_count)
    out_table = tables[0].reshape(row_total, features)
    input_table = tables[1].reshape(row_total, features)

    source = slots // per_split
    step = 2 * my_core - 1
    ring_offset = ((source // 2 - my_z) * step) % ring
    other_core = (source % 2) ^ my_core
    slot_of = jnp.where(
        ring_offset == 0,
        other_core,
        jnp.where(
            ring_offset == 1,
            2 + other_core,
            jnp.where(ring_offset == 2, 4 + 3 * other_core, 6 - other_core),
        ),
    )
    table_row = (slot_of * expert_count + flat_routes) * per_split + slots % per_split
    gather = table_row[:, None] == jnp.arange(row_total, dtype=jnp.int32)[None, :]
    out_pairs = select_rows(gather, out_table).reshape(token_count, TOP, features)
    input_pairs = select_rows(gather, input_table).reshape(token_count, TOP, features)
    grad_values = out_grad.astype(jnp.float32)
    mixed = jnp.sum(combine_weights[:, :, None] * out_pairs, axis=1).astype(jnp.bfloat16)
    combine_grad = jnp.sum(grad_values[:, None, :] * out_pairs, axis=2)
    tokens_grad = jnp.sum(input_pairs, axis=1).astype(jnp.bfloat16)
    return (
        mixed,
        tokens_grad,
        combine_grad,
        gate_weight_grad[None],
        up_weight_grad[None],
        down_weight_grad[None],
    )


def solution(mesh):
    return jax.shard_map(
        shards,
        mesh=mesh,
        in_specs=(
            P("expert", None),
            P("expert", None),
            P("expert", None),
            P("expert", None),
            P("expert", None, "etp"),
            P("expert", None, "etp"),
            P("expert", "etp", None),
        ),
        out_specs=(
            P("expert", None),
            P("expert", None),
            P("expert", None),
            P("expert", None, "etp"),
            P("expert", None, "etp"),
            P("expert", "etp", None),
        ),
        check_vma=False,
    )
```

```python
import jax
import jax.numpy as jnp
from jax import lax
from jax.sharding import PartitionSpec as P

TOP = 2


def contract_last(left, right):
    return lax.dot_general(
        left, right, (((1,), (1,)), ((), ())), preferred_element_type=jnp.float32
    )


def contract_first(left, right):
    return lax.dot_general(
        left, right, (((0,), (0,)), ((), ())), preferred_element_type=jnp.float32
    )


def select_rows(selector, table):
    return jnp.dot(selector.astype(table.dtype), table, preferred_element_type=jnp.float32)


def expert_rows(rows_in, rows_grad, gate_w, up_w, down_w):
    gate_pre = jnp.dot(rows_in, gate_w, preferred_element_type=jnp.float32)
    up_pre = jnp.dot(rows_in, up_w, preferred_element_type=jnp.float32)
    gate_sig = jax.nn.sigmoid(gate_pre)
    swish = gate_pre * gate_sig
    hidden = (swish * up_pre).astype(jnp.bfloat16)
    out_part = jnp.dot(hidden, down_w, preferred_element_type=jnp.float32)
    hidden_grad = contract_last(rows_grad, down_w)
    gate_grad = (hidden_grad * up_pre * gate_sig * (1.0 + gate_pre * (1.0 - gate_sig))).astype(
        jnp.bfloat16
    )
    up_grad = (hidden_grad * swish).astype(jnp.bfloat16)
    input_part = contract_last(gate_grad, gate_w) + contract_last(up_grad, up_w)
    return out_part, input_part, hidden, gate_grad, up_grad


def etp_perms(split_count):
    ring = split_count // 2
    swap = [(i, i ^ 1) for i in range(split_count)]
    onward = [(i, ((i // 2 + 1 - 2 * (i % 2)) % ring) * 2 + i % 2) for i in range(split_count)]
    backward = [(target, source) for source, target in onward]
    return swap, onward, backward


def etp_gather(unit, split_count, cover=None):
    swap, onward, _ = etp_perms(split_count)
    chip = jnp.stack([unit, lax.ppermute(unit, "etp", swap)], axis=1)
    first = lax.ppermute(chip, "etp", onward)
    if cover is not None:
        first, cover = lax.optimization_barrier((first, cover))
    second = lax.ppermute(first[:, 0], "etp", onward)
    first_other = lax.ppermute(first, "etp", swap)
    second_other = lax.ppermute(second, "etp", swap)
    return jnp.concatenate(
        [chip, first, second[:, None], first_other, second_other[:, None]], axis=1
    ), cover


def etp_reduce(part, split_count, cover_near=None, cover_far=None):
    swap, _, backward = etp_perms(split_count)

    def send(value, perm):
        return lax.ppermute(value.astype(jnp.bfloat16), "etp", perm).astype(jnp.float32)

    held = part[2:5] + send(part[5:8], swap)
    arrived = send(held[2], backward)
    arrived, cover_near = lax.optimization_barrier((arrived, cover_near))
    near = held[0] + arrived
    arrived = send(jnp.stack([near, held[1]], axis=0), backward)
    arrived, cover_far = lax.optimization_barrier((arrived, cover_far))
    chip = part[0:2] + arrived
    return chip[0] + send(chip[1], swap), cover_near, cover_far


def shards(tokens, out_grad, routes, combine_weights, w_gate, w_up, w_down):
    expert_count = lax.axis_size("expert")
    split_count = lax.axis_size("etp")
    ring = split_count // 2
    me = lax.axis_index("etp")
    my_z = me // 2
    my_core = me % 2
    token_count, features = tokens.shape
    capacity = token_count // 4
    per_split = capacity // split_count
    pair_count = token_count * TOP

    flat_routes = routes.reshape(pair_count)
    expert_hot = (flat_routes[:, None] == jnp.arange(expert_count, dtype=jnp.int32)[None, :]).astype(
        jnp.int32
    )
    before = jnp.cumsum(expert_hot, axis=0) - expert_hot
    slots = jnp.sum(before * expert_hot, axis=1)

    mine = (slots // per_split) == me
    local_place = jnp.where(mine, flat_routes * per_split + slots % per_split, -1)
    place_count = expert_count * per_split
    pick = local_place[None, :] == jnp.arange(place_count, dtype=jnp.int32)[:, None]
    pick_tokens = jnp.any(pick.reshape(place_count, token_count, TOP), axis=2)

    send_rows = select_rows(pick_tokens, tokens).astype(jnp.bfloat16)
    place_weight = jnp.sum(jnp.where(pick, combine_weights.reshape(1, pair_count), 0.0), axis=1)
    send_grad = (place_weight[:, None] * select_rows(pick_tokens, out_grad)).astype(jnp.bfloat16)
    send = jnp.concatenate([send_rows, send_grad], axis=1).reshape(
        expert_count, per_split, 2 * features
    )
    recv = lax.all_to_all(send, "expert", split_axis=0, concat_axis=0, tiled=True)
    unit = recv.reshape(place_count, 2 * features)

    swap, onward, _ = etp_perms(split_count)
    weights = (w_gate[0], w_up[0], w_down[0])
    chip = jnp.stack([unit, lax.ppermute(unit, "etp", swap)], axis=0)
    first = lax.ppermute(chip, "etp", onward)
    pieces = [chip.reshape(2 * place_count, 2 * features)]
    results = [expert_rows(pieces[0][:, :features], pieces[0][:, features:], *weights)]
    first, results[0] = lax.optimization_barrier((first, results[0]))
    second = lax.ppermute(first[0], "etp", onward)
    first_other = lax.ppermute(first, "etp", swap)
    pieces.append(jnp.concatenate([first, first_other], axis=0).reshape(4 * place_count, 2 * features))
    results.append(expert_rows(pieces[1][:, :features], pieces[1][:, features:], *weights))
    second, results[1] = lax.optimization_barrier((second, results[1]))
    second_other = lax.ppermute(second, "etp", swap)
    pieces.append(jnp.concatenate([second, second_other], axis=0))
    results.append(expert_rows(pieces[2][:, :features], pieces[2][:, features:], *weights))

    rows_in = jnp.concatenate([piece[:, :features] for piece in pieces], axis=0)
    rows_grad = jnp.concatenate([piece[:, features:] for piece in pieces], axis=0)
    hidden, gate_grad, up_grad = (
        jnp.concatenate(parts, axis=0) for parts in list(zip(*results))[2:]
    )
    pair_rows = 2 * place_count
    out_part, input_part = (
        jnp.concatenate(
            [
                parts[0],
                parts[1][:pair_rows],
                parts[2][:place_count],
                parts[1][pair_rows:],
                parts[2][place_count:],
            ],
            axis=0,
        )
        for parts in list(zip(*results))[:2]
    )
    row_total = split_count * place_count

    block = (split_count, 1, place_count, features)
    sums, down_weight_grad, (gate_weight_grad, up_weight_grad) = etp_reduce(
        jnp.concatenate(
            [
                out_part.astype(jnp.bfloat16).astype(jnp.float32).reshape(block),
                input_part.astype(jnp.bfloat16).astype(jnp.float32).reshape(block),
            ],
            axis=1,
        ),
        split_count,
        contract_first(hidden, rows_grad).astype(jnp.bfloat16),
        (
            contract_first(rows_in, gate_grad).astype(jnp.bfloat16),
            contract_first(rows_in, up_grad).astype(jnp.bfloat16),
        ),
    )
    sums = sums.astype(jnp.bfloat16)
    back = jnp.concatenate(
        [
            sums[0].reshape(expert_count, per_split, features),
            sums[1].reshape(expert_count, per_split, features),
        ],
        axis=1,
    )
    back = lax.all_to_all(back, "expert", split_axis=0, concat_axis=0, tiled=True)
    back = back.reshape(expert_count, 2, per_split, features).transpose(1, 0, 2, 3)
    tables, _ = etp_gather(back.reshape(2, place_count, features), split_count)
    out_table = tables[0].reshape(row_total, features)
    input_table = tables[1].reshape(row_total, features)

    source = slots // per_split
    step = 2 * my_core - 1
    ring_offset = ((source // 2 - my_z) * step) % ring
    other_core = (source % 2) ^ my_core
    slot_of = jnp.where(
        ring_offset == 0,
        other_core,
        jnp.where(
            ring_offset == 1,
            2 + other_core,
            jnp.where(ring_offset == 2, 4 + 3 * other_core, 6 - other_core),
        ),
    )
    table_row = (slot_of * expert_count + flat_routes) * per_split + slots % per_split
    gather = table_row[:, None] == jnp.arange(row_total, dtype=jnp.int32)[None, :]
    out_pairs = select_rows(gather, out_table).reshape(token_count, TOP, features)
    input_pairs = select_rows(gather, input_table).reshape(token_count, TOP, features)
    grad_values = out_grad.astype(jnp.float32)
    mixed = jnp.sum(combine_weights[:, :, None] * out_pairs, axis=1).astype(jnp.bfloat16)
    combine_grad = jnp.sum(grad_values[:, None, :] * out_pairs, axis=2)
    tokens_grad = jnp.sum(input_pairs, axis=1).astype(jnp.bfloat16)
    return (
        mixed,
        tokens_grad,
        combine_grad,
        gate_weight_grad[None],
        up_weight_grad[None],
        down_weight_grad[None],
    )


def solution(mesh):
    return jax.shard_map(
        shards,
        mesh=mesh,
        in_specs=(
            P("expert", None),
            P("expert", None),
            P("expert", None),
            P("expert", None),
            P("expert", None, "etp"),
            P("expert", None, "etp"),
            P("expert", "etp", None),
        ),
        out_specs=(
            P("expert", None),
            P("expert", None),
            P("expert", None),
            P("expert", None, "etp"),
            P("expert", None, "etp"),
            P("expert", "etp", None),
        ),
        check_vma=False,
    )
```

```python
import jax
import jax.numpy as jnp
from jax import lax
from jax.sharding import PartitionSpec as P

TOP = 2


def contract_last(left, right):
    return lax.dot_general(
        left, right, (((1,), (1,)), ((), ())), preferred_element_type=jnp.float32
    )


def contract_first(left, right):
    return lax.dot_general(
        left, right, (((0,), (0,)), ((), ())), preferred_element_type=jnp.float32
    )


def select_rows(selector, table):
    return jnp.dot(selector.astype(table.dtype), table, preferred_element_type=jnp.float32)


def expert_rows(rows_in, rows_grad, gate_w, up_w, down_w):
    gate_pre = jnp.dot(rows_in, gate_w, preferred_element_type=jnp.float32)
    up_pre = jnp.dot(rows_in, up_w, preferred_element_type=jnp.float32)
    gate_sig = jax.nn.sigmoid(gate_pre)
    swish = gate_pre * gate_sig
    hidden = (swish * up_pre).astype(jnp.bfloat16)
    out_part = jnp.dot(hidden, down_w, preferred_element_type=jnp.float32)
    hidden_grad = contract_last(rows_grad, down_w)
    gate_grad = (hidden_grad * up_pre * gate_sig * (1.0 + gate_pre * (1.0 - gate_sig))).astype(
        jnp.bfloat16
    )
    up_grad = (hidden_grad * swish).astype(jnp.bfloat16)
    input_part = contract_last(gate_grad, gate_w) + contract_last(up_grad, up_w)
    return out_part, input_part, hidden, gate_grad, up_grad


def etp_perms(split_count):
    ring = split_count // 2
    swap = [(i, i ^ 1) for i in range(split_count)]
    onward = [(i, ((i // 2 + 1 - 2 * (i % 2)) % ring) * 2 + i % 2) for i in range(split_count)]
    backward = [(target, source) for source, target in onward]
    return swap, onward, backward


def etp_gather(unit, split_count, cover=None):
    swap, onward, _ = etp_perms(split_count)
    chip = jnp.stack([unit, lax.ppermute(unit, "etp", swap)], axis=1)
    first = lax.ppermute(chip, "etp", onward)
    if cover is not None:
        first, cover = lax.optimization_barrier((first, cover))
    second = lax.ppermute(first[:, 0], "etp", onward)
    first_other = lax.ppermute(first, "etp", swap)
    second_other = lax.ppermute(second, "etp", swap)
    return jnp.concatenate(
        [chip, first, second[:, None], first_other, second_other[:, None]], axis=1
    ), cover


def etp_reduce(part, split_count, cover_near=None, cover_far=None):
    swap, _, backward = etp_perms(split_count)

    def send(value, perm):
        return lax.ppermute(value.astype(jnp.bfloat16), "etp", perm).astype(jnp.float32)

    pair = send(jnp.stack([part[5], part[6]], axis=0), swap)
    arrived = send(part[4] + send(part[7], swap), backward)
    arrived, cover_near = lax.optimization_barrier((arrived, cover_near))
    near = part[2] + pair[0] + arrived
    arrived = send(jnp.stack([near, part[3] + pair[1]], axis=0), backward)
    arrived, cover_far = lax.optimization_barrier((arrived, cover_far))
    chip = jnp.stack([part[0], part[1]], axis=0) + arrived
    return chip[0] + send(chip[1], swap), cover_near, cover_far


def shards(tokens, out_grad, routes, combine_weights, w_gate, w_up, w_down):
    expert_count = lax.axis_size("expert")
    split_count = lax.axis_size("etp")
    ring = split_count // 2
    me = lax.axis_index("etp")
    my_z = me // 2
    my_core = me % 2
    token_count, features = tokens.shape
    capacity = token_count // 4
    per_split = capacity // split_count
    pair_count = token_count * TOP

    flat_routes = routes.reshape(pair_count)
    expert_hot = (flat_routes[:, None] == jnp.arange(expert_count, dtype=jnp.int32)[None, :]).astype(
        jnp.int32
    )
    before = jnp.cumsum(expert_hot, axis=0) - expert_hot
    slots = jnp.sum(before * expert_hot, axis=1)

    mine = (slots // per_split) == me
    local_place = jnp.where(mine, flat_routes * per_split + slots % per_split, -1)
    place_count = expert_count * per_split
    pick = local_place[None, :] == jnp.arange(place_count, dtype=jnp.int32)[:, None]
    pick_tokens = jnp.any(pick.reshape(place_count, token_count, TOP), axis=2)

    send_rows = select_rows(pick_tokens, tokens).astype(jnp.bfloat16)
    place_weight = jnp.sum(jnp.where(pick, combine_weights.reshape(1, pair_count), 0.0), axis=1)
    send_grad = (place_weight[:, None] * select_rows(pick_tokens, out_grad)).astype(jnp.bfloat16)
    send = jnp.concatenate([send_rows, send_grad], axis=1).reshape(
        expert_count, per_split, 2 * features
    )
    recv = lax.all_to_all(send, "expert", split_axis=0, concat_axis=0, tiled=True)
    unit = recv.reshape(place_count, 2 * features)

    swap, onward, _ = etp_perms(split_count)
    weights = (w_gate[0], w_up[0], w_down[0])
    chip = jnp.stack([unit, lax.ppermute(unit, "etp", swap)], axis=0)
    first = lax.ppermute(chip, "etp", onward)
    pieces = [chip.reshape(2 * place_count, 2 * features)]
    results = [expert_rows(pieces[0][:, :features], pieces[0][:, features:], *weights)]
    first, results[0] = lax.optimization_barrier((first, results[0]))
    second = lax.ppermute(first[0], "etp", onward)
    first_other = lax.ppermute(first, "etp", swap)
    pieces.append(jnp.concatenate([first, first_other], axis=0).reshape(4 * place_count, 2 * features))
    results.append(expert_rows(pieces[1][:, :features], pieces[1][:, features:], *weights))
    second, results[1] = lax.optimization_barrier((second, results[1]))
    second_other = lax.ppermute(second, "etp", swap)
    pieces.append(jnp.concatenate([second, second_other], axis=0))
    results.append(expert_rows(pieces[2][:, :features], pieces[2][:, features:], *weights))

    rows_in = jnp.concatenate([piece[:, :features] for piece in pieces], axis=0)
    rows_grad = jnp.concatenate([piece[:, features:] for piece in pieces], axis=0)
    hidden, gate_grad, up_grad = (
        jnp.concatenate(parts, axis=0) for parts in list(zip(*results))[2:]
    )
    chunk_slots = ((0, 1), (2, 3, 5, 6), (4, 7))
    part = [None] * split_count
    for slots_of_chunk, result in zip(chunk_slots, results):
        for index, slot in enumerate(slots_of_chunk):
            rows = slice(index * place_count, (index + 1) * place_count)
            part[slot] = jnp.stack(
                [
                    result[0][rows].astype(jnp.bfloat16).astype(jnp.float32),
                    result[1][rows].astype(jnp.bfloat16).astype(jnp.float32),
                ],
                axis=0,
            )
    row_total = split_count * place_count

    sums, down_weight_grad, (gate_weight_grad, up_weight_grad) = etp_reduce(
        part,
        split_count,
        contract_first(hidden, rows_grad).astype(jnp.bfloat16),
        (
            contract_first(rows_in, gate_grad).astype(jnp.bfloat16),
            contract_first(rows_in, up_grad).astype(jnp.bfloat16),
        ),
    )
    sums = sums.astype(jnp.bfloat16)
    back = jnp.concatenate(
        [
            sums[0].reshape(expert_count, per_split, features),
            sums[1].reshape(expert_count, per_split, features),
        ],
        axis=1,
    )
    back = lax.all_to_all(back, "expert", split_axis=0, concat_axis=0, tiled=True)
    back = back.reshape(expert_count, 2, per_split, features).transpose(1, 0, 2, 3)
    tables, _ = etp_gather(back.reshape(2, place_count, features), split_count)
    out_table = tables[0].reshape(row_total, features)
    input_table = tables[1].reshape(row_total, features)

    source = slots // per_split
    step = 2 * my_core - 1
    ring_offset = ((source // 2 - my_z) * step) % ring
    other_core = (source % 2) ^ my_core
    slot_of = jnp.where(
        ring_offset == 0,
        other_core,
        jnp.where(
            ring_offset == 1,
            2 + other_core,
            jnp.where(ring_offset == 2, 4 + 3 * other_core, 6 - other_core),
        ),
    )
    table_row = (slot_of * expert_count + flat_routes) * per_split + slots % per_split
    gather = table_row[:, None] == jnp.arange(row_total, dtype=jnp.int32)[None, :]
    out_pairs = select_rows(gather, out_table).reshape(token_count, TOP, features)
    input_pairs = select_rows(gather, input_table).reshape(token_count, TOP, features)
    grad_values = out_grad.astype(jnp.float32)
    mixed = jnp.sum(combine_weights[:, :, None] * out_pairs, axis=1).astype(jnp.bfloat16)
    combine_grad = jnp.sum(grad_values[:, None, :] * out_pairs, axis=2)
    tokens_grad = jnp.sum(input_pairs, axis=1).astype(jnp.bfloat16)
    return (
        mixed,
        tokens_grad,
        combine_grad,
        gate_weight_grad[None],
        up_weight_grad[None],
        down_weight_grad[None],
    )


def solution(mesh):
    return jax.shard_map(
        shards,
        mesh=mesh,
        in_specs=(
            P("expert", None),
            P("expert", None),
            P("expert", None),
            P("expert", None),
            P("expert", None, "etp"),
            P("expert", None, "etp"),
            P("expert", "etp", None),
        ),
        out_specs=(
            P("expert", None),
            P("expert", None),
            P("expert", None),
            P("expert", None, "etp"),
            P("expert", None, "etp"),
            P("expert", "etp", None),
        ),
        check_vma=False,
    )
```

```python
import jax
import jax.numpy as jnp
from jax import lax
from jax.sharding import PartitionSpec as P

TOP = 2


def contract_last(left, right):
    return lax.dot_general(
        left, right, (((1,), (1,)), ((), ())), preferred_element_type=jnp.float32
    )


def contract_first(left, right):
    return lax.dot_general(
        left, right, (((0,), (0,)), ((), ())), preferred_element_type=jnp.float32
    )


def select_rows(selector, table):
    return jnp.dot(selector.astype(table.dtype), table, preferred_element_type=jnp.float32)


def expert_rows(rows_in, rows_grad, gate_w, up_w, down_w):
    gate_pre = jnp.dot(rows_in, gate_w, preferred_element_type=jnp.float32)
    up_pre = jnp.dot(rows_in, up_w, preferred_element_type=jnp.float32)
    gate_sig = jax.nn.sigmoid(gate_pre)
    swish = gate_pre * gate_sig
    hidden = (swish * up_pre).astype(jnp.bfloat16)
    out_part = jnp.dot(hidden, down_w, preferred_element_type=jnp.float32)
    hidden_grad = contract_last(rows_grad, down_w)
    gate_grad = (hidden_grad * up_pre * gate_sig * (1.0 + gate_pre * (1.0 - gate_sig))).astype(
        jnp.bfloat16
    )
    up_grad = (hidden_grad * swish).astype(jnp.bfloat16)
    input_part = contract_last(gate_grad, gate_w) + contract_last(up_grad, up_w)
    return out_part, input_part, hidden, gate_grad, up_grad


def etp_perms(split_count):
    ring = split_count // 2
    swap = [(i, i ^ 1) for i in range(split_count)]
    onward = [(i, ((i // 2 + 1 - 2 * (i % 2)) % ring) * 2 + i % 2) for i in range(split_count)]
    backward = [(target, source) for source, target in onward]
    return swap, onward, backward


def etp_gather(unit, split_count, cover=None):
    swap, onward, _ = etp_perms(split_count)
    chip = jnp.stack([unit, lax.ppermute(unit, "etp", swap)], axis=1)
    first = lax.ppermute(chip, "etp", onward)
    if cover is not None:
        first, cover = lax.optimization_barrier((first, cover))
    second = lax.ppermute(first[:, 0], "etp", onward)
    first_other = lax.ppermute(first, "etp", swap)
    second_other = lax.ppermute(second, "etp", swap)
    return jnp.concatenate(
        [chip, first, second[:, None], first_other, second_other[:, None]], axis=1
    ), cover


def etp_reduce(part, split_count, cover_near=None, cover_far=None, pair=None):
    swap, _, backward = etp_perms(split_count)

    def send(value, perm):
        return lax.ppermute(value.astype(jnp.bfloat16), "etp", perm).astype(jnp.float32)

    if pair is None:
        pair = send(jnp.stack([part[5], part[6]], axis=0), swap)
    arrived = send(part[4] + send(part[7], swap), backward)
    arrived, cover_near = lax.optimization_barrier((arrived, cover_near))
    near = part[2] + pair[0] + arrived
    arrived = send(jnp.stack([near, part[3] + pair[1]], axis=0), backward)
    arrived, cover_far = lax.optimization_barrier((arrived, cover_far))
    chip = jnp.stack([part[0], part[1]], axis=0) + arrived
    return chip[0] + send(chip[1], swap), cover_near, cover_far


def shards(tokens, out_grad, routes, combine_weights, w_gate, w_up, w_down):
    expert_count = lax.axis_size("expert")
    split_count = lax.axis_size("etp")
    ring = split_count // 2
    me = lax.axis_index("etp")
    my_z = me // 2
    my_core = me % 2
    token_count, features = tokens.shape
    capacity = token_count // 4
    per_split = capacity // split_count
    pair_count = token_count * TOP

    flat_routes = routes.reshape(pair_count)
    expert_hot = (flat_routes[:, None] == jnp.arange(expert_count, dtype=jnp.int32)[None, :]).astype(
        jnp.int32
    )
    before = jnp.cumsum(expert_hot, axis=0) - expert_hot
    slots = jnp.sum(before * expert_hot, axis=1)

    mine = (slots // per_split) == me
    local_place = jnp.where(mine, flat_routes * per_split + slots % per_split, -1)
    place_count = expert_count * per_split
    pick = local_place[None, :] == jnp.arange(place_count, dtype=jnp.int32)[:, None]
    pick_tokens = jnp.any(pick.reshape(place_count, token_count, TOP), axis=2)

    send_rows = select_rows(pick_tokens, tokens).astype(jnp.bfloat16)
    place_weight = jnp.sum(jnp.where(pick, combine_weights.reshape(1, pair_count), 0.0), axis=1)
    send_grad = (place_weight[:, None] * select_rows(pick_tokens, out_grad)).astype(jnp.bfloat16)
    send = jnp.concatenate([send_rows, send_grad], axis=1).reshape(
        expert_count, per_split, 2 * features
    )
    recv = lax.all_to_all(send, "expert", split_axis=0, concat_axis=0, tiled=True)
    unit = recv.reshape(place_count, 2 * features)

    swap, onward, _ = etp_perms(split_count)
    weights = (w_gate[0], w_up[0], w_down[0])
    chip = jnp.stack([unit, lax.ppermute(unit, "etp", swap)], axis=0)
    first = lax.ppermute(chip, "etp", onward)
    pieces = [chip.reshape(2 * place_count, 2 * features)]
    results = [expert_rows(pieces[0][:, :features], pieces[0][:, features:], *weights)]
    first, results[0] = lax.optimization_barrier((first, results[0]))
    second = lax.ppermute(first[0], "etp", onward)
    first_other = lax.ppermute(first, "etp", swap)
    pieces.append(jnp.concatenate([first, first_other], axis=0).reshape(4 * place_count, 2 * features))
    results.append(expert_rows(pieces[1][:, :features], pieces[1][:, features:], *weights))
    second, results[1] = lax.optimization_barrier((second, results[1]))
    partner_rows = slice(2 * place_count, 4 * place_count)
    pair = lax.ppermute(
        jnp.stack(
            [
                part_rows.astype(jnp.bfloat16)[partner_rows].reshape(2, place_count, features)
                for part_rows in results[1][:2]
            ],
            axis=1,
        ),
        "etp",
        swap,
    ).astype(jnp.float32)
    second_other = lax.ppermute(second, "etp", swap)
    pieces.append(jnp.concatenate([second, second_other], axis=0))
    results.append(expert_rows(pieces[2][:, :features], pieces[2][:, features:], *weights))
    pair, results[2] = lax.optimization_barrier((pair, results[2]))

    rows_in = jnp.concatenate([piece[:, :features] for piece in pieces], axis=0)
    rows_grad = jnp.concatenate([piece[:, features:] for piece in pieces], axis=0)
    hidden, gate_grad, up_grad = (
        jnp.concatenate(parts, axis=0) for parts in list(zip(*results))[2:]
    )
    chunk_slots = ((0, 1), (2, 3, 5, 6), (4, 7))
    part = [None] * split_count
    for slots_of_chunk, result in zip(chunk_slots, results):
        for index, slot in enumerate(slots_of_chunk):
            rows = slice(index * place_count, (index + 1) * place_count)
            part[slot] = jnp.stack(
                [
                    result[0][rows].astype(jnp.bfloat16).astype(jnp.float32),
                    result[1][rows].astype(jnp.bfloat16).astype(jnp.float32),
                ],
                axis=0,
            )
    row_total = split_count * place_count

    sums, down_weight_grad, (gate_weight_grad, up_weight_grad) = etp_reduce(
        part,
        split_count,
        contract_first(hidden, rows_grad).astype(jnp.bfloat16),
        (
            contract_first(rows_in, gate_grad).astype(jnp.bfloat16),
            contract_first(rows_in, up_grad).astype(jnp.bfloat16),
        ),
        pair,
    )
    sums = sums.astype(jnp.bfloat16)
    back = jnp.concatenate(
        [
            sums[0].reshape(expert_count, per_split, features),
            sums[1].reshape(expert_count, per_split, features),
        ],
        axis=1,
    )
    back = lax.all_to_all(back, "expert", split_axis=0, concat_axis=0, tiled=True)
    back = back.reshape(expert_count, 2, per_split, features).transpose(1, 0, 2, 3)
    tables, _ = etp_gather(back.reshape(2, place_count, features), split_count)
    out_table = tables[0].reshape(row_total, features)
    input_table = tables[1].reshape(row_total, features)

    source = slots // per_split
    step = 2 * my_core - 1
    ring_offset = ((source // 2 - my_z) * step) % ring
    other_core = (source % 2) ^ my_core
    slot_of = jnp.where(
        ring_offset == 0,
        other_core,
        jnp.where(
            ring_offset == 1,
            2 + other_core,
            jnp.where(ring_offset == 2, 4 + 3 * other_core, 6 - other_core),
        ),
    )
    table_row = (slot_of * expert_count + flat_routes) * per_split + slots % per_split
    gather = table_row[:, None] == jnp.arange(row_total, dtype=jnp.int32)[None, :]
    out_pairs = select_rows(gather, out_table).reshape(token_count, TOP, features)
    input_pairs = select_rows(gather, input_table).reshape(token_count, TOP, features)
    grad_values = out_grad.astype(jnp.float32)
    mixed = jnp.sum(combine_weights[:, :, None] * out_pairs, axis=1).astype(jnp.bfloat16)
    combine_grad = jnp.sum(grad_values[:, None, :] * out_pairs, axis=2)
    tokens_grad = jnp.sum(input_pairs, axis=1).astype(jnp.bfloat16)
    return (
        mixed,
        tokens_grad,
        combine_grad,
        gate_weight_grad[None],
        up_weight_grad[None],
        down_weight_grad[None],
    )


def solution(mesh):
    return jax.shard_map(
        shards,
        mesh=mesh,
        in_specs=(
            P("expert", None),
            P("expert", None),
            P("expert", None),
            P("expert", None),
            P("expert", None, "etp"),
            P("expert", None, "etp"),
            P("expert", "etp", None),
        ),
        out_specs=(
            P("expert", None),
            P("expert", None),
            P("expert", None),
            P("expert", None, "etp"),
            P("expert", None, "etp"),
            P("expert", "etp", None),
        ),
        check_vma=False,
    )
```

```python
import jax
import jax.numpy as jnp
from jax import lax
from jax.sharding import PartitionSpec as P

TOP = 2


def contract_last(left, right):
    return lax.dot_general(
        left, right, (((1,), (1,)), ((), ())), preferred_element_type=jnp.float32
    )


def contract_first(left, right):
    return lax.dot_general(
        left, right, (((0,), (0,)), ((), ())), preferred_element_type=jnp.float32
    )


def select_rows(selector, table):
    return jnp.dot(selector.astype(table.dtype), table, preferred_element_type=jnp.float32)


def expert_rows(rows_in, rows_grad, gate_w, up_w, down_w):
    gate_pre = jnp.dot(rows_in, gate_w, preferred_element_type=jnp.float32)
    up_pre = jnp.dot(rows_in, up_w, preferred_element_type=jnp.float32)
    gate_sig = jax.nn.sigmoid(gate_pre)
    swish = gate_pre * gate_sig
    hidden = (swish * up_pre).astype(jnp.bfloat16)
    out_part = jnp.dot(hidden, down_w, preferred_element_type=jnp.float32)
    hidden_grad = contract_last(rows_grad, down_w)
    gate_grad = (hidden_grad * up_pre * gate_sig * (1.0 + gate_pre * (1.0 - gate_sig))).astype(
        jnp.bfloat16
    )
    up_grad = (hidden_grad * swish).astype(jnp.bfloat16)
    input_part = contract_last(gate_grad, gate_w) + contract_last(up_grad, up_w)
    return out_part, input_part, hidden, gate_grad, up_grad


def etp_perms(split_count):
    ring = split_count // 2
    swap = [(i, i ^ 1) for i in range(split_count)]
    onward = [(i, ((i // 2 + 1 - 2 * (i % 2)) % ring) * 2 + i % 2) for i in range(split_count)]
    backward = [(target, source) for source, target in onward]
    return swap, onward, backward


def etp_gather(unit, split_count, cover=None):
    swap, onward, _ = etp_perms(split_count)
    chip = jnp.stack([unit, lax.ppermute(unit, "etp", swap)], axis=1)
    first = lax.ppermute(chip, "etp", onward)
    if cover is not None:
        first, cover = lax.optimization_barrier((first, cover))
    second = lax.ppermute(first[:, 0], "etp", onward)
    first_other = lax.ppermute(first, "etp", swap)
    second_other = lax.ppermute(second, "etp", swap)
    return jnp.concatenate(
        [chip, first, second[:, None], first_other, second_other[:, None]], axis=1
    ), cover


def etp_reduce(part, split_count, cover_near=None, cover_far=None):
    swap, _, backward = etp_perms(split_count)

    def send(value, perm):
        return lax.ppermute(value.astype(jnp.bfloat16), "etp", perm).astype(jnp.float32)

    pair = send(jnp.stack([part[5], part[6]], axis=0), swap)
    arrived = send(part[4] + send(part[7], swap), backward)
    arrived, cover_near = lax.optimization_barrier((arrived, cover_near))
    near = part[2] + pair[0] + arrived
    arrived = send(jnp.stack([near, part[3] + pair[1]], axis=0), backward)
    arrived, cover_far = lax.optimization_barrier((arrived, cover_far))
    chip = jnp.stack([part[0], part[1]], axis=0) + arrived
    return chip[0] + send(chip[1], swap), cover_near, cover_far


def shards(tokens, out_grad, routes, combine_weights, w_gate, w_up, w_down):
    expert_count = lax.axis_size("expert")
    split_count = lax.axis_size("etp")
    ring = split_count // 2
    me = lax.axis_index("etp")
    my_z = me // 2
    my_core = me % 2
    token_count, features = tokens.shape
    capacity = token_count // 4
    per_split = capacity // split_count
    pair_count = token_count * TOP

    flat_routes = routes.reshape(pair_count)
    expert_hot = (flat_routes[:, None] == jnp.arange(expert_count, dtype=jnp.int32)[None, :]).astype(
        jnp.int32
    )
    before = jnp.cumsum(expert_hot, axis=0) - expert_hot
    slots = jnp.sum(before * expert_hot, axis=1)

    mine = (slots // per_split) == me
    local_place = jnp.where(mine, flat_routes * per_split + slots % per_split, -1)
    place_count = expert_count * per_split
    pick = local_place[None, :] == jnp.arange(place_count, dtype=jnp.int32)[:, None]
    pick_tokens = jnp.any(pick.reshape(place_count, token_count, TOP), axis=2)

    place_weight = jnp.sum(jnp.where(pick, combine_weights.reshape(1, pair_count), 0.0), axis=1)
    picked = select_rows(pick_tokens, jnp.concatenate([tokens, out_grad], axis=1))
    send = jnp.concatenate(
        [picked[:, :features], place_weight[:, None] * picked[:, features:]], axis=1
    ).astype(jnp.bfloat16).reshape(expert_count, per_split, 2 * features)
    recv = lax.all_to_all(send, "expert", split_axis=0, concat_axis=0, tiled=True)
    unit = recv.reshape(place_count, 2 * features)

    swap, onward, _ = etp_perms(split_count)
    weights = (w_gate[0], w_up[0], w_down[0])
    chip = jnp.stack([unit, lax.ppermute(unit, "etp", swap)], axis=0)
    first = lax.ppermute(chip, "etp", onward)
    pieces = [chip.reshape(2 * place_count, 2 * features)]
    results = [expert_rows(pieces[0][:, :features], pieces[0][:, features:], *weights)]
    first, results[0] = lax.optimization_barrier((first, results[0]))
    second = lax.ppermute(first[0], "etp", onward)
    first_other = lax.ppermute(first, "etp", swap)
    pieces.append(jnp.concatenate([first, first_other], axis=0).reshape(4 * place_count, 2 * features))
    results.append(expert_rows(pieces[1][:, :features], pieces[1][:, features:], *weights))
    second, results[1] = lax.optimization_barrier((second, results[1]))
    second_other = lax.ppermute(second, "etp", swap)
    pieces.append(jnp.concatenate([second, second_other], axis=0))
    results.append(expert_rows(pieces[2][:, :features], pieces[2][:, features:], *weights))

    rows_in = jnp.concatenate([piece[:, :features] for piece in pieces], axis=0)
    rows_grad = jnp.concatenate([piece[:, features:] for piece in pieces], axis=0)
    hidden, gate_grad, up_grad = (
        jnp.concatenate(parts, axis=0) for parts in list(zip(*results))[2:]
    )
    chunk_slots = ((0, 1), (2, 3, 5, 6), (4, 7))
    part = [None] * split_count
    for slots_of_chunk, result in zip(chunk_slots, results):
        for index, slot in enumerate(slots_of_chunk):
            rows = slice(index * place_count, (index + 1) * place_count)
            part[slot] = jnp.stack(
                [
                    result[0][rows].astype(jnp.bfloat16).astype(jnp.float32),
                    result[1][rows].astype(jnp.bfloat16).astype(jnp.float32),
                ],
                axis=0,
            )
    row_total = split_count * place_count

    sums, down_weight_grad, (gate_weight_grad, up_weight_grad) = etp_reduce(
        part,
        split_count,
        contract_first(hidden, rows_grad).astype(jnp.bfloat16),
        (
            contract_first(rows_in, gate_grad).astype(jnp.bfloat16),
            contract_first(rows_in, up_grad).astype(jnp.bfloat16),
        ),
    )
    sums = sums.astype(jnp.bfloat16)
    back = jnp.concatenate(
        [
            sums[0].reshape(expert_count, per_split, features),
            sums[1].reshape(expert_count, per_split, features),
        ],
        axis=1,
    )
    back = lax.all_to_all(back, "expert", split_axis=0, concat_axis=0, tiled=True)
    back = back.reshape(expert_count, 2, per_split, features).transpose(1, 0, 2, 3)
    tables, _ = etp_gather(back.reshape(2, place_count, features), split_count)
    out_table = tables[0].reshape(row_total, features)
    input_table = tables[1].reshape(row_total, features)

    source = slots // per_split
    step = 2 * my_core - 1
    ring_offset = ((source // 2 - my_z) * step) % ring
    other_core = (source % 2) ^ my_core
    slot_of = jnp.where(
        ring_offset == 0,
        other_core,
        jnp.where(
            ring_offset == 1,
            2 + other_core,
            jnp.where(ring_offset == 2, 4 + 3 * other_core, 6 - other_core),
        ),
    )
    table_row = (slot_of * expert_count + flat_routes) * per_split + slots % per_split
    gather = table_row[:, None] == jnp.arange(row_total, dtype=jnp.int32)[None, :]
    out_pairs = select_rows(gather, out_table).reshape(token_count, TOP, features)
    grad_values = out_grad.astype(jnp.float32)
    mixed = jnp.sum(combine_weights[:, :, None] * out_pairs, axis=1).astype(jnp.bfloat16)
    combine_grad = jnp.sum(grad_values[:, None, :] * out_pairs, axis=2)
    token_gather = jnp.any(gather.reshape(token_count, TOP, row_total), axis=1)
    tokens_grad = select_rows(token_gather, input_table).astype(jnp.bfloat16)
    return (
        mixed,
        tokens_grad,
        combine_grad,
        gate_weight_grad[None],
        up_weight_grad[None],
        down_weight_grad[None],
    )


def solution(mesh):
    return jax.shard_map(
        shards,
        mesh=mesh,
        in_specs=(
            P("expert", None),
            P("expert", None),
            P("expert", None),
            P("expert", None),
            P("expert", None, "etp"),
            P("expert", None, "etp"),
            P("expert", "etp", None),
        ),
        out_specs=(
            P("expert", None),
            P("expert", None),
            P("expert", None),
            P("expert", None, "etp"),
            P("expert", None, "etp"),
            P("expert", "etp", None),
        ),
        check_vma=False,
    )
```
